32 devices in a mesh: groups: 2 (over x), row: 8 (over z, y), col: 2 (over core).
Axes of the slice: x: 2, y: 2, z: 4, core: 2. Of those that a mesh axis runs over, the one named last changes fastest.
Arguments:
- tokens: bfloat16 [512, 16384], P(('groups', 'col'), 'row'), parts along dimension 0, may hold values from -6 to 6
- q_weight: bfloat16 [16384, 8192], P('row', 'col'), may hold values from -0.046875 to 0.046875
- key_matrix: bfloat16 [16384, 512], P('row', 'col'), may hold values from -0.046875 to 0.046875
- value_matrix: bfloat16 [16384, 512], P('row', 'col'), may hold values from -0.046875 to 0.046875
- o_weight: bfloat16 [8192, 16384], P('col', 'row'), may hold values from -0.0625 to 0.0625
- k_cache: bfloat16 [32, 1536, 4, 128], P(('groups', 'row'), None, 'col'), parts along dimension 0, may hold values from -200 to 200
- value_cache: bfloat16 [32, 1536, 4, 128], P(('groups', 'row'), None, 'col'), parts along dimension 0, may hold values from -6 to 6
- cache_len: int32 [32], P('groups'), parts along dimension 0, may hold values from 1 to 1536, 12288 in all
- slot_seq: int32 [32], P('groups'), parts along dimension 0, may hold values from 0 to 15, each once
Outputs:
- layer_out: bfloat16 [512, 16384], P(('groups', 'col'), 'row'), parts along dimension 0
The draws below stay inside these ranges and needn't reach their ends.
There are 2 independent parts, one for each index of `groups`. The reference program is written for one: setup_inputs(seed, part) draws one part's arguments, and reference() takes and returns one part's arrays. A program takes and returns all parts, laid end to end along the dimension named above; an argument that names none is the same for every part. Nothing has to cross between parts.
Inputs may be any that keep to these rules, and one draw needn't show every extreme that they name: `cache_len`: every sequence has at least one cached token and at most 1536; some sequence has exactly 1536. `slot_seq`: each sequence stands in exactly one slot.
All inputs are finite; a program needn't handle non-finite values.
Results may differ from the reference program's by a relative error of at most 0.038.
Values may be sent and summed in bfloat16 or wider, within the bound.
No kernel may reach another device: no remote copies, remote signals or barrier semaphores. Data moves between devices by JAX's collectives and lax.ppermute only.
A program may use at most 128 MiB of HBM per device.

```python
import math
import jax
import jax.numpy as jnp
import numpy as np
from jax import lax

MODEL_WIDTH = 16384
HQ = 64
KEY_VALUE_HEADS = 4
HEAD_SIZE = 128
NEW = 16
SLOT_TOKEN_LIMIT = 1536
SEQUENCE_COUNT = 16
SPAN_TOKENS = 256
N_ROW = 8


def draw_k_cache(key, part):
    drawn_key_rows = jnp.clip(jax.random.normal(key, (SEQUENCE_COUNT, SLOT_TOKEN_LIMIT, KEY_VALUE_HEADS, HEAD_SIZE), jnp.float32), -5.0, 5.0)
    return drawn_key_rows.astype(jnp.bfloat16)


def levels(key, shape, cuts, smallest, largest):
    def one(position, blocks):
        steps = jax.random.uniform(jax.random.fold_in(jax.random.fold_in(key, 6), position), (blocks,), jnp.float32, smallest / len(cuts), largest / len(cuts))
        return jnp.repeat(jnp.exp(steps), shape[position] // blocks).reshape((-1,) + (1,) * (len(shape) - position - 1))

    factor_of = one(*cuts[0])
    for cut in cuts[1:]:
        factor_of = factor_of * one(*cut)
    return factor_of


def profile(count, total, bound, skew):
    portions = [(1 << 20) // math.isqrt(grade ** skew) + 1 for grade in range(2, count + 1)]
    surplus, holding = total - bound - (count - 1), [1] * (count - 1)
    while surplus > 0:
        free = [i for i in range(count - 1) if holding[i] < bound]
        mass, budget = sum([portions[i] for i in free]), surplus
        for i in free:
            extra = min(bound - holding[i], max(1, budget * portions[i] // mass), surplus)
            holding[i] = holding[i] + extra
            surplus = surplus - extra
    return np.array([bound] + holding)


def uneven(own_key, count, total, limit, lean):
    if count == 2:
        one = jax.random.randint(own_key, (), max(1, total - limit), min(limit, total - 1) + 1)
        return jnp.stack([one, total - one])
    lengths = jnp.asarray(profile(count, total, limit, lean), jnp.int32)
    twos = (count - 1) // 2
    giver, receiver = lengths[1:1 + 2 * twos:2], lengths[2:2 + 2 * twos:2]
    margin = jnp.minimum(giver - 1, limit - receiver)
    moved = jax.random.randint(jax.random.fold_in(own_key, 1), (twos,), 0, 1 << 20) % (margin + 1)
    lengths = lengths.at[1:1 + 2 * twos:2].set(giver - moved).at[2:2 + 2 * twos:2].set(receiver + moved)
    return lengths[jax.random.permutation(jax.random.fold_in(own_key, 2), count)]


def scatter_about(stream_key, shape, scale, limit, cuts=(), kind=jnp.bfloat16):
    gain = levels(stream_key, shape, cuts, -0.22, 0.18) if cuts else 1.0
    result = jax.random.normal(stream_key, shape, jnp.float32) * scale * gain
    return jnp.minimum(jnp.maximum(result, -limit), limit).astype(kind)


def setup_inputs(seed: int = 0, part: int = 0) -> dict:
    streams_of = jax.random.split(jax.random.key(seed), 10)
    own_keys = jax.random.split(jax.random.fold_in(streams_of[9], part), 10)
    return {
        "tokens": scatter_about(own_keys[0], (SPAN_TOKENS, MODEL_WIDTH), 1.0, 6.0, ((0, 2), (1, 8))),
        "q_weight": scatter_about(streams_of[1], (MODEL_WIDTH, HQ * HEAD_SIZE), MODEL_WIDTH ** -0.5, 0.046875, ((0, 8), (1, 2))),
        "key_matrix": scatter_about(streams_of[2], (MODEL_WIDTH, KEY_VALUE_HEADS * HEAD_SIZE), MODEL_WIDTH ** -0.5, 0.046875, ((0, 8), (1, 2))),
        "value_matrix": scatter_about(streams_of[3], (MODEL_WIDTH, KEY_VALUE_HEADS * HEAD_SIZE), MODEL_WIDTH ** -0.5, 0.046875, ((0, 8), (1, 2))),
        "o_weight": scatter_about(streams_of[4], (HQ * HEAD_SIZE, MODEL_WIDTH), (HQ * HEAD_SIZE) ** -0.5, 0.0625, ((0, 2), (1, 8))),
        "k_cache": draw_k_cache(jax.random.fold_in(jax.random.fold_in(streams_of[9], part), 71), part),
        "value_cache": scatter_about(own_keys[6], (SEQUENCE_COUNT, SLOT_TOKEN_LIMIT, KEY_VALUE_HEADS, HEAD_SIZE), 1.0, 6.0, ((0, 8), (2, 2))),
        "cache_len": uneven(own_keys[7], SEQUENCE_COUNT, SEQUENCE_COUNT * SLOT_TOKEN_LIMIT // 2, SLOT_TOKEN_LIMIT, 2).astype(jnp.int32),
        "slot_seq": jax.random.permutation(own_keys[8], SEQUENCE_COUNT).astype(jnp.int32),
    }


ROPE_BASE = 500000.0

def apply_turning(values, token_places):
    half_dim = values.shape[-1] // 2
    frequency = ROPE_BASE ** (-(2.0 * jnp.arange(half_dim, dtype=jnp.float32)) / values.shape[-1])
    angles = token_places[:, None] * frequency[None, :]
    cosine = jnp.cos(angles)[:, None, :]
    sine_part = jnp.sin(angles)[:, None, :]
    leading = values[..., :half_dim]
    trailing = values[..., half_dim:]
    return jnp.concatenate([leading * cosine - trailing * sine_part, trailing * cosine + leading * sine_part], axis=-1)

def attend(queries, incoming_keys, incoming_values, cached_keys, cached_values, length):
    tokens_new, kv_heads, head_dim = incoming_keys.shape
    grouped = queries.reshape(tokens_new, kv_heads, -1, head_dim).astype(jnp.float32)
    scale_factor = 1.0 / math.sqrt(head_dim)
    cache_scores = jnp.einsum('nkgd,ckd->kgnc', grouped, cached_keys.astype(jnp.float32)) * scale_factor
    valid_cache = jnp.arange(cached_keys.shape[0]) < length
    cache_scores = jnp.where(valid_cache, cache_scores, -jnp.inf)
    fresh_scores = jnp.einsum('nkgd,mkd->kgnm', grouped, incoming_keys.astype(jnp.float32)) * scale_factor
    causal = jnp.arange(tokens_new)[None, :] <= jnp.arange(tokens_new)[:, None]
    fresh_scores = jnp.where(causal, fresh_scores, -jnp.inf)
    highest = jnp.maximum(lax.optimization_barrier(jnp.max(cache_scores, axis=-1)), lax.optimization_barrier(jnp.max(fresh_scores, axis=-1)))
    cache_weights = jnp.exp(cache_scores - highest[..., None])
    fresh_weights = jnp.exp(fresh_scores - highest[..., None])
    totals = lax.optimization_barrier(jnp.sum(cache_weights, axis=-1)) + lax.optimization_barrier(jnp.sum(fresh_weights, axis=-1))
    cache_rounded = cache_weights.astype(jnp.bfloat16).astype(jnp.float32)
    fresh_rounded = fresh_weights.astype(jnp.bfloat16).astype(jnp.float32)
    weighted = jnp.einsum('kgnc,ckd->nkgd', cache_rounded, cached_values.astype(jnp.float32))
    weighted = weighted + jnp.einsum('kgnm,mkd->nkgd', fresh_rounded, incoming_values.astype(jnp.float32))
    normed = weighted / jnp.transpose(totals, (2, 0, 1))[..., None]
    return normed.reshape(tokens_new, -1).astype(jnp.bfloat16)

def reference(tokens, q_weight, key_matrix, value_matrix, o_weight, k_cache, value_cache, cache_len, slot_seq):
    block_width = MODEL_WIDTH // N_ROW

    def block_step(carry, block_index):
        first_col = (block_index * block_width).astype(jnp.int32)
        rows_block = lax.dynamic_slice_in_dim(tokens, first_col, block_width, 1)
        results = []
        for running, weight in zip(carry, (q_weight, key_matrix, value_matrix)):
            block_term = jnp.dot(rows_block, lax.dynamic_slice_in_dim(weight, first_col, block_width, 0), preferred_element_type=jnp.float32)
            rounded = lax.optimization_barrier(block_term.astype(jnp.bfloat16))
            results.append(running + rounded.astype(jnp.float32))
        return (tuple(results), None)
    initial = (jnp.zeros((SPAN_TOKENS, q_weight.shape[1]), jnp.float32), jnp.zeros((SPAN_TOKENS, key_matrix.shape[1]), jnp.float32), jnp.zeros((SPAN_TOKENS, value_matrix.shape[1]), jnp.float32))
    summed, _ = lax.scan(block_step, initial, jnp.arange(N_ROW, dtype=jnp.int32))
    q_sum, key_total_sum, value_total_sum = summed
    token_places = (cache_len[:, None] + jnp.arange(NEW, dtype=jnp.int32)[None, :]).reshape(-1).astype(jnp.float32)
    queries = apply_turning(q_sum.reshape(SPAN_TOKENS, HQ, HEAD_SIZE), token_places).astype(jnp.bfloat16)
    incoming_keys = apply_turning(key_total_sum.reshape(SPAN_TOKENS, KEY_VALUE_HEADS, HEAD_SIZE), token_places).astype(jnp.bfloat16)
    incoming_values = value_total_sum.reshape(SPAN_TOKENS, KEY_VALUE_HEADS, HEAD_SIZE).astype(jnp.bfloat16)
    matches = (slot_seq[:, None] == jnp.arange(SEQUENCE_COUNT, dtype=jnp.int32)[None, :]).astype(jnp.int32)
    slot_of = lax.optimization_barrier(jnp.sum(matches * jnp.arange(SEQUENCE_COUNT, dtype=jnp.int32)[:, None], axis=0)).astype(jnp.int32)

    def per_sequence(seq_index):
        first_row = (seq_index * NEW).astype(jnp.int32)
        q_rows = lax.dynamic_slice_in_dim(queries, first_row, NEW, 0)
        k_rows = lax.dynamic_slice_in_dim(incoming_keys, first_row, NEW, 0)
        v_rows = lax.dynamic_slice_in_dim(incoming_values, first_row, NEW, 0)
        slot_index = slot_of[seq_index]
        cached_keys = lax.dynamic_index_in_dim(k_cache, slot_index, 0, keepdims=False)
        cached_values = lax.dynamic_index_in_dim(value_cache, slot_index, 0, keepdims=False)
        return attend(q_rows, k_rows, v_rows, cached_keys, cached_values, cache_len[seq_index])
    attended = lax.map(per_sequence, jnp.arange(SEQUENCE_COUNT, dtype=jnp.int32)).reshape(SPAN_TOKENS, HQ * HEAD_SIZE)
    return jnp.dot(attended, o_weight, preferred_element_type=jnp.float32).astype(jnp.bfloat16)
```

```python
import math

import jax
import jax.numpy as jnp
from jax import lax
from jax.sharding import PartitionSpec as P

ROPE_BASE = 500000.0


def apply_turning(values, token_places):
    half_dim = values.shape[-1] // 2
    frequency = ROPE_BASE ** (-(2.0 * jnp.arange(half_dim, dtype=jnp.float32)) / values.shape[-1])
    angles = token_places[:, None] * frequency[None, :]
    cosine = jnp.cos(angles)[:, None, :]
    sine_part = jnp.sin(angles)[:, None, :]
    leading = values[..., :half_dim]
    trailing = values[..., half_dim:]
    return jnp.concatenate(
        [leading * cosine - trailing * sine_part, trailing * cosine + leading * sine_part], axis=-1
    )


def attend(queries, incoming_keys, incoming_values, cached_keys, cached_values, length):
    tokens_new, kv_heads, head_dim = incoming_keys.shape
    grouped = queries.reshape(tokens_new, kv_heads, -1, head_dim)
    scale_factor = 1.0 / math.sqrt(head_dim)
    cache_scores = (
        jnp.einsum("nkgd,ckd->kgnc", grouped, cached_keys, preferred_element_type=jnp.float32)
        * scale_factor
    )
    valid_cache = jnp.arange(cached_keys.shape[0]) < length
    cache_scores = jnp.where(valid_cache, cache_scores, -jnp.inf)
    fresh_scores = (
        jnp.einsum("nkgd,mkd->kgnm", grouped, incoming_keys, preferred_element_type=jnp.float32)
        * scale_factor
    )
    causal = jnp.arange(tokens_new)[None, :] <= jnp.arange(tokens_new)[:, None]
    fresh_scores = jnp.where(causal, fresh_scores, -jnp.inf)
    highest = jnp.maximum(jnp.max(cache_scores, axis=-1), jnp.max(fresh_scores, axis=-1))
    cache_weights = jnp.exp(cache_scores - highest[..., None])
    fresh_weights = jnp.exp(fresh_scores - highest[..., None])
    totals = jnp.sum(cache_weights, axis=-1) + jnp.sum(fresh_weights, axis=-1)
    weighted = jnp.einsum(
        "kgnc,ckd->nkgd",
        cache_weights.astype(jnp.bfloat16),
        cached_values,
        preferred_element_type=jnp.float32,
    )
    weighted = weighted + jnp.einsum(
        "kgnm,mkd->nkgd",
        fresh_weights.astype(jnp.bfloat16),
        incoming_values,
        preferred_element_type=jnp.float32,
    )
    normed = weighted / jnp.transpose(totals, (2, 0, 1))[..., None]
    return normed.reshape(tokens_new, -1).astype(jnp.bfloat16)


def body(
    tokens, q_weight, key_matrix, value_matrix, o_weight, k_cache, value_cache, cache_len, slot_seq
):
    row_index = lax.axis_index("row")
    seq_dev = k_cache.shape[0]
    head_dim = k_cache.shape[3]
    slot_total = slot_seq.shape[0]
    gathered = lax.all_gather(tokens, "col", axis=0, tiled=True)
    new_len = gathered.shape[0] // slot_total
    slot_list = jnp.arange(slot_total)
    sequences = slot_seq[slot_list]
    row_ids = (sequences[:, None] * new_len + jnp.arange(new_len)[None, :]).reshape(-1)
    chosen = gathered[row_ids]
    q_part = jnp.dot(chosen, q_weight, preferred_element_type=jnp.float32)
    k_part = jnp.dot(chosen, key_matrix, preferred_element_type=jnp.float32)
    v_part = jnp.dot(chosen, value_matrix, preferred_element_type=jnp.float32)
    q_part, k_part, v_part = (q_part, k_part, v_part)
    q_width = q_part.shape[1]
    k_width = k_part.shape[1]
    joined = jnp.concatenate(
        [q_part.astype(jnp.bfloat16), k_part.astype(jnp.bfloat16), v_part.astype(jnp.bfloat16)],
        axis=1,
    )
    summed = lax.psum_scatter(joined, "row", scatter_dimension=0, tiled=True).astype(jnp.float32)
    q_sum = summed[:, :q_width]
    key_total_sum = summed[:, q_width : q_width + k_width]
    value_total_sum = summed[:, q_width + k_width :]
    local_slots = row_index * seq_dev + jnp.arange(seq_dev)
    sequences = slot_seq[local_slots]
    starts = cache_len[sequences]
    token_places = (starts[:, None] + jnp.arange(new_len)[None, :]).reshape(-1).astype(jnp.float32)
    row_total = q_sum.shape[0]
    queries = apply_turning(q_sum.reshape(row_total, -1, head_dim), token_places).astype(
        jnp.bfloat16
    )
    rotated_keys = apply_turning(
        key_total_sum.reshape(row_total, -1, head_dim), token_places
    ).astype(jnp.bfloat16)
    values = value_total_sum.reshape(row_total, -1, head_dim).astype(jnp.bfloat16)
    results = jax.vmap(attend)(
        queries.reshape(seq_dev, new_len, -1, head_dim),
        rotated_keys.reshape(seq_dev, new_len, -1, head_dim),
        values.reshape(seq_dev, new_len, -1, head_dim),
        k_cache,
        value_cache,
        starts,
    )
    attended = results.reshape(seq_dev * new_len, -1)
    products = jnp.dot(
        lax.all_gather(attended, "row", axis=0, tiled=True),
        o_weight,
        preferred_element_type=jnp.float32,
    )
    matches = (slot_seq[:, None] == jnp.arange(slot_total)[None, :]).astype(jnp.int32)
    slot_of = jnp.sum(matches * jnp.arange(slot_total)[:, None], axis=0)
    row_order = (slot_of[:, None] * new_len + jnp.arange(new_len)[None, :]).reshape(-1)
    ordered = products[row_order]
    return lax.psum_scatter(ordered.astype(jnp.bfloat16), "col", scatter_dimension=0, tiled=True)


def solution(mesh):
    return jax.shard_map(
        body,
        mesh=mesh,
        in_specs=(
            P(("groups", "col"), "row"),
            P("row", "col"),
            P("row", "col"),
            P("row", "col"),
            P("col", "row"),
            P(("groups", "row"), None, "col", None),
            P(("groups", "row"), None, "col", None),
            P("groups"),
            P("groups"),
        ),
        out_specs=P(("groups", "col"), "row"),
        check_vma=False,
    )
```

```python
import math

import jax
import jax.numpy as jnp
import numpy as np
from jax import lax
from jax.sharding import PartitionSpec as P

ROPE_BASE = 500000.0


def apply_turning(values, token_places):
    half_dim = values.shape[-1] // 2
    frequency = ROPE_BASE ** (-(2.0 * jnp.arange(half_dim, dtype=jnp.float32)) / values.shape[-1])
    angles = token_places[:, None] * frequency[None, :]
    cosine = jnp.cos(angles)[:, None, :]
    sine_part = jnp.sin(angles)[:, None, :]
    leading = values[..., :half_dim]
    trailing = values[..., half_dim:]
    return jnp.concatenate(
        [leading * cosine - trailing * sine_part, trailing * cosine + leading * sine_part], axis=-1
    )


def attend(queries, incoming_keys, incoming_values, cached_keys, cached_values, length):
    tokens_new, kv_heads, head_dim = incoming_keys.shape
    grouped = queries.reshape(tokens_new, kv_heads, -1, head_dim)
    scale_factor = 1.0 / math.sqrt(head_dim)
    cache_scores = (
        jnp.einsum("nkgd,ckd->kgnc", grouped, cached_keys, preferred_element_type=jnp.float32)
        * scale_factor
    )
    valid_cache = jnp.arange(cached_keys.shape[0]) < length
    cache_scores = jnp.where(valid_cache, cache_scores, -jnp.inf)
    fresh_scores = (
        jnp.einsum("nkgd,mkd->kgnm", grouped, incoming_keys, preferred_element_type=jnp.float32)
        * scale_factor
    )
    causal = jnp.arange(tokens_new)[None, :] <= jnp.arange(tokens_new)[:, None]
    fresh_scores = jnp.where(causal, fresh_scores, -jnp.inf)
    highest = jnp.maximum(jnp.max(cache_scores, axis=-1), jnp.max(fresh_scores, axis=-1))
    cache_weights = jnp.exp(cache_scores - highest[..., None])
    fresh_weights = jnp.exp(fresh_scores - highest[..., None])
    totals = jnp.sum(cache_weights, axis=-1) + jnp.sum(fresh_weights, axis=-1)
    weighted = jnp.einsum(
        "kgnc,ckd->nkgd",
        cache_weights.astype(jnp.bfloat16),
        cached_values,
        preferred_element_type=jnp.float32,
    )
    weighted = weighted + jnp.einsum(
        "kgnm,mkd->nkgd",
        fresh_weights.astype(jnp.bfloat16),
        incoming_values,
        preferred_element_type=jnp.float32,
    )
    normed = weighted / jnp.transpose(totals, (2, 0, 1))[..., None]
    return normed.reshape(tokens_new, -1).astype(jnp.bfloat16)


def row_ring(mesh):
    n_row = mesh.shape["row"]
    natural = list(range(n_row))
    try:
        names = list(mesh.axis_names)
        picked = np.moveaxis(np.asarray(mesh.devices), names.index("row"), 0).reshape(n_row, -1)[:, 0]
        coords = [tuple(d.coords) for d in picked]
    except Exception:
        return natural
    varying = [a for a in range(len(coords[0])) if len({c[a] for c in coords}) > 1]
    if len(varying) != 2:
        return natural
    sizes = {a: len({c[a] for c in coords}) for a in varying}
    inner = [a for a in varying if sizes[a] == 2]
    if not inner or sizes[varying[0]] * sizes[varying[1]] != n_row:
        return natural
    inner = inner[-1]
    outer = [a for a in varying if a != inner][0]
    lo, hi = min(c[inner] for c in coords), max(c[inner] for c in coords)
    first = sorted([i for i in natural if coords[i][inner] == lo], key=lambda i: coords[i][outer])
    second = sorted([i for i in natural if coords[i][inner] == hi], key=lambda i: -coords[i][outer])
    return first + second


def make_body(ring):
    n_row = len(ring)
    position_of = [ring.index(i) for i in range(n_row)]
    forward_hops = n_row // 2
    backward_hops = n_row - 1 - forward_hops
    forward_pairs = [(ring[i], ring[(i + 1) % n_row]) for i in range(n_row)]
    backward_pairs = [(ring[i], ring[(i - 1) % n_row]) for i in range(n_row)]
    gather_offsets = [0]
    for s in range(forward_hops):
        gather_offsets.append(-(s + 1) % n_row)
        if s < backward_hops:
            gather_offsets.append((s + 1) % n_row)
    stacked_of_offset = [gather_offsets.index(d) for d in range(n_row)]

    def add_bf16(a, b):
        return (a.astype(jnp.float32) + b.astype(jnp.float32)).astype(jnp.bfloat16)

    def ring_reduce_scatter(blocks):
        if n_row == 1:
            return blocks[0].astype(jnp.float32)
        forward = blocks[forward_hops % n_row]
        backward = blocks[(n_row - backward_hops) % n_row] if backward_hops else None
        got_forward = got_backward = None
        for s in range(forward_hops):
            got_forward = lax.ppermute(forward, "row", forward_pairs)
            if s < backward_hops:
                got_backward = lax.ppermute(backward, "row", backward_pairs)
            if s < forward_hops - 1:
                forward = add_bf16(got_forward, blocks[(forward_hops - s - 1) % n_row])
            if s < backward_hops - 1:
                backward = add_bf16(got_backward, blocks[(s + 1 - backward_hops) % n_row])
        total = got_forward.astype(jnp.float32) + blocks[0].astype(jnp.float32)
        if got_backward is not None:
            total = total + got_backward.astype(jnp.float32)
        return total

    def ring_all_gather(own):
        got = [own]
        forward = backward = own
        for s in range(forward_hops):
            forward = lax.ppermute(forward, "row", forward_pairs)
            got.append(forward)
            if s < backward_hops:
                backward = lax.ppermute(backward, "row", backward_pairs)
                got.append(backward)
        return jnp.concatenate(got, axis=0)

    def body(
        tokens, q_weight, key_matrix, value_matrix, o_weight, k_cache, value_cache, cache_len, slot_seq
    ):
        row_index = lax.axis_index("row")
        col_index = lax.axis_index("col")
        n_col = 2
        seq_dev = k_cache.shape[0]
        head_dim = k_cache.shape[3]
        slot_total = slot_seq.shape[0]
        own_rows = tokens.shape[0]
        other_tokens = lax.ppermute(tokens, "col", [(0, 1), (1, 0)])
        both = jnp.concatenate([tokens, other_tokens], axis=0)
        new_len = own_rows * n_col // slot_total
        my_pos = jnp.asarray(position_of, jnp.int32)[row_index]
        ring_arr = jnp.asarray(ring, jnp.int32)
        block_dev = ring_arr[(my_pos + jnp.arange(n_row)) % n_row]
        slots = (block_dev[:, None] * seq_dev + jnp.arange(seq_dev)[None, :]).reshape(-1)
        sequences = slot_seq[slots]
        token_rows = (sequences[:, None] * new_len + jnp.arange(new_len)[None, :]).reshape(-1)
        local_rows = jnp.where(
            token_rows // own_rows == col_index, token_rows % own_rows, own_rows + token_rows % own_rows
        )
        chosen = both[local_rows]
        q_part = jnp.dot(chosen, q_weight, preferred_element_type=jnp.float32)
        k_part = jnp.dot(chosen, key_matrix, preferred_element_type=jnp.float32)
        v_part = jnp.dot(chosen, value_matrix, preferred_element_type=jnp.float32)
        q_width = q_part.shape[1]
        k_width = k_part.shape[1]
        joined = jnp.concatenate(
            [q_part.astype(jnp.bfloat16), k_part.astype(jnp.bfloat16), v_part.astype(jnp.bfloat16)],
            axis=1,
        )
        block_rows = seq_dev * new_len
        blocks = [joined[k * block_rows : (k + 1) * block_rows] for k in range(n_row)]
        summed = ring_reduce_scatter(blocks)
        q_sum = summed[:, :q_width]
        key_total_sum = summed[:, q_width : q_width + k_width]
        value_total_sum = summed[:, q_width + k_width :]
        local_slots = row_index * seq_dev + jnp.arange(seq_dev)
        starts = cache_len[slot_seq[local_slots]]
        token_places = (starts[:, None] + jnp.arange(new_len)[None, :]).reshape(-1).astype(jnp.float32)
        row_total = q_sum.shape[0]
        queries = apply_turning(q_sum.reshape(row_total, -1, head_dim), token_places).astype(
            jnp.bfloat16
        )
        rotated_keys = apply_turning(
            key_total_sum.reshape(row_total, -1, head_dim), token_places
        ).astype(jnp.bfloat16)
        values = value_total_sum.reshape(row_total, -1, head_dim).astype(jnp.bfloat16)
        results = jax.vmap(attend)(
            queries.reshape(seq_dev, new_len, -1, head_dim),
            rotated_keys.reshape(seq_dev, new_len, -1, head_dim),
            values.reshape(seq_dev, new_len, -1, head_dim),
            k_cache,
            value_cache,
            starts,
        )
        attended = results.reshape(seq_dev * new_len, -1)
        products = jnp.dot(ring_all_gather(attended), o_weight, preferred_element_type=jnp.float32)
        matches = (slot_seq[:, None] == jnp.arange(slot_total)[None, :]).astype(jnp.int32)
        slot_of = jnp.sum(matches * jnp.arange(slot_total)[:, None], axis=0)
        span = jnp.arange(own_rows * n_col)
        seq_of = span // new_len
        slot_t = slot_of[seq_of]
        offset = (jnp.asarray(position_of, jnp.int32)[slot_t // seq_dev] - my_pos) % n_row
        stacked = jnp.asarray(stacked_of_offset, jnp.int32)[offset]
        product_rows = stacked * block_rows + (slot_t % seq_dev) * new_len + span % new_len
        product_rows = product_rows.reshape(n_col, own_rows)
        mine = products[lax.dynamic_index_in_dim(product_rows, col_index, 0, keepdims=False)]
        theirs = products[lax.dynamic_index_in_dim(product_rows, 1 - col_index, 0, keepdims=False)]
        received = lax.ppermute(theirs.astype(jnp.bfloat16), "col", [(0, 1), (1, 0)])
        return (mine + received.astype(jnp.float32)).astype(jnp.bfloat16)

    return body


def solution(mesh):
    return jax.shard_map(
        make_body(row_ring(mesh)),
        mesh=mesh,
        in_specs=(
            P(("groups", "col"), "row"),
            P("row", "col"),
            P("row", "col"),
            P("row", "col"),
            P("col", "row"),
            P(("groups", "row"), None, "col", None),
            P(("groups", "row"), None, "col", None),
            P("groups"),
            P("groups"),
        ),
        out_specs=P(("groups", "col"), "row"),
        check_vma=False,
    )
```

```python
import math

import jax
import jax.numpy as jnp
import numpy as np
from jax import lax
from jax.sharding import PartitionSpec as P

ROPE_BASE = 500000.0


def apply_turning(values, token_places):
    half_dim = values.shape[-1] // 2
    frequency = ROPE_BASE ** (-(2.0 * jnp.arange(half_dim, dtype=jnp.float32)) / values.shape[-1])
    angles = token_places[:, None] * frequency[None, :]
    cosine = jnp.cos(angles)[:, None, :]
    sine_part = jnp.sin(angles)[:, None, :]
    leading = values[..., :half_dim]
    trailing = values[..., half_dim:]
    return jnp.concatenate(
        [leading * cosine - trailing * sine_part, trailing * cosine + leading * sine_part], axis=-1
    )


def attend(queries, incoming_keys, incoming_values, cached_keys, cached_values, length):
    tokens_new, kv_heads, head_dim = incoming_keys.shape
    grouped = queries.reshape(tokens_new, kv_heads, -1, head_dim)
    scale_factor = 1.0 / math.sqrt(head_dim)
    cache_scores = (
        jnp.einsum("nkgd,ckd->kgnc", grouped, cached_keys, preferred_element_type=jnp.float32)
        * scale_factor
    )
    valid_cache = jnp.arange(cached_keys.shape[0]) < length
    cache_scores = jnp.where(valid_cache, cache_scores, -jnp.inf)
    fresh_scores = (
        jnp.einsum("nkgd,mkd->kgnm", grouped, incoming_keys, preferred_element_type=jnp.float32)
        * scale_factor
    )
    causal = jnp.arange(tokens_new)[None, :] <= jnp.arange(tokens_new)[:, None]
    fresh_scores = jnp.where(causal, fresh_scores, -jnp.inf)
    highest = jnp.maximum(jnp.max(cache_scores, axis=-1), jnp.max(fresh_scores, axis=-1))
    cache_weights = jnp.exp(cache_scores - highest[..., None])
    fresh_weights = jnp.exp(fresh_scores - highest[..., None])
    totals = jnp.sum(cache_weights, axis=-1) + jnp.sum(fresh_weights, axis=-1)
    weighted = jnp.einsum(
        "kgnc,ckd->nkgd",
        cache_weights.astype(jnp.bfloat16),
        cached_values,
        preferred_element_type=jnp.float32,
    )
    weighted = weighted + jnp.einsum(
        "kgnm,mkd->nkgd",
        fresh_weights.astype(jnp.bfloat16),
        incoming_values,
        preferred_element_type=jnp.float32,
    )
    normed = weighted / jnp.transpose(totals, (2, 0, 1))[..., None]
    return normed.reshape(tokens_new, -1).astype(jnp.bfloat16)


def row_ring(mesh):
    n_row = mesh.shape["row"]
    natural = list(range(n_row))
    try:
        names = list(mesh.axis_names)
        picked = np.moveaxis(np.asarray(mesh.devices), names.index("row"), 0).reshape(n_row, -1)[:, 0]
        coords = [tuple(d.coords) for d in picked]
    except Exception:
        return natural
    varying = [a for a in range(len(coords[0])) if len({c[a] for c in coords}) > 1]
    if len(varying) != 2:
        return natural
    sizes = {a: len({c[a] for c in coords}) for a in varying}
    inner = [a for a in varying if sizes[a] == 2]
    if not inner or sizes[varying[0]] * sizes[varying[1]] != n_row:
        return natural
    inner = inner[-1]
    outer = [a for a in varying if a != inner][0]
    lo, hi = min(c[inner] for c in coords), max(c[inner] for c in coords)
    first = sorted([i for i in natural if coords[i][inner] == lo], key=lambda i: coords[i][outer])
    second = sorted([i for i in natural if coords[i][inner] == hi], key=lambda i: -coords[i][outer])
    return first + second


def make_body(ring):
    n_row = len(ring)
    position_of = [ring.index(i) for i in range(n_row)]
    forward_hops = n_row // 2
    backward_hops = n_row - 1 - forward_hops
    forward_pairs = [(ring[i], ring[(i + 1) % n_row]) for i in range(n_row)]
    backward_pairs = [(ring[i], ring[(i - 1) % n_row]) for i in range(n_row)]
    gather_offsets = [0]
    for s in range(forward_hops):
        gather_offsets.append(-(s + 1) % n_row)
        if s < backward_hops:
            gather_offsets.append((s + 1) % n_row)
    stacked_of_offset = [gather_offsets.index(d) for d in range(n_row)]

    def add_bf16(a, b):
        return (a.astype(jnp.float32) + b.astype(jnp.float32)).astype(jnp.bfloat16)

    def ring_reduce_scatter(blocks):
        if n_row == 1:
            return blocks[0].astype(jnp.float32)
        forward = blocks[forward_hops % n_row]
        backward = blocks[(n_row - backward_hops) % n_row] if backward_hops else None
        got_forward = got_backward = None
        for s in range(forward_hops):
            got_forward = lax.ppermute(forward, "row", forward_pairs)
            if s < backward_hops:
                got_backward = lax.ppermute(backward, "row", backward_pairs)
            if s < forward_hops - 1:
                forward = add_bf16(got_forward, blocks[(forward_hops - s - 1) % n_row])
            if s < backward_hops - 1:
                backward = add_bf16(got_backward, blocks[(s + 1 - backward_hops) % n_row])
        total = got_forward.astype(jnp.float32) + blocks[0].astype(jnp.float32)
        if got_backward is not None:
            total = total + got_backward.astype(jnp.float32)
        return total

    def ring_all_gather(own):
        got = [own]
        forward = backward = own
        for s in range(forward_hops):
            forward = lax.ppermute(forward, "row", forward_pairs)
            got.append(forward)
            if s < backward_hops:
                backward = lax.ppermute(backward, "row", backward_pairs)
                got.append(backward)
        return jnp.concatenate(got, axis=0)

    def lookup(table, index):
        table = jnp.asarray(table, jnp.int32)
        hit = index[..., None] == jnp.arange(table.shape[0], dtype=jnp.int32)
        return jnp.sum(jnp.where(hit, table, 0), axis=-1)

    def one_hot(rows, width):
        return (rows[:, None] == jnp.arange(width, dtype=jnp.int32)[None, :]).astype(jnp.bfloat16)

    def body(
        tokens, q_weight, key_matrix, value_matrix, o_weight, k_cache, value_cache, cache_len, slot_seq
    ):
        row_index = lax.axis_index("row").astype(jnp.int32)
        col_index = lax.axis_index("col").astype(jnp.int32)
        n_col = 2
        seq_dev = k_cache.shape[0]
        head_dim = k_cache.shape[3]
        slot_total = slot_seq.shape[0]
        own_rows = tokens.shape[0]
        span_rows = own_rows * n_col
        new_len = span_rows // slot_total
        block_rows = seq_dev * new_len
        other_tokens = lax.ppermute(tokens, "col", [(0, 1), (1, 0)])
        my_pos = lookup(position_of, row_index)
        block_dev = lookup(ring, (my_pos + jnp.arange(n_row, dtype=jnp.int32)) % n_row)
        slots = (block_dev[:, None] * seq_dev + jnp.arange(seq_dev, dtype=jnp.int32)[None, :]).reshape(-1)
        sequences = lookup(slot_seq, slots)
        local = jnp.arange(span_rows, dtype=jnp.int32)
        token_rows = jnp.repeat(sequences, new_len) * new_len + local % new_len
        from_own = token_rows // own_rows == col_index
        in_half = token_rows % own_rows
        pick_own = one_hot(jnp.where(from_own, in_half, -1), own_rows)
        pick_other = one_hot(jnp.where(from_own, -1, in_half), own_rows)
        chosen = (
            jnp.dot(pick_own, tokens, preferred_element_type=jnp.float32)
            + jnp.dot(pick_other, other_tokens, preferred_element_type=jnp.float32)
        ).astype(jnp.bfloat16)
        q_part = jnp.dot(chosen, q_weight, preferred_element_type=jnp.float32)
        k_part = jnp.dot(chosen, key_matrix, preferred_element_type=jnp.float32)
        v_part = jnp.dot(chosen, value_matrix, preferred_element_type=jnp.float32)
        q_width = q_part.shape[1]
        k_width = k_part.shape[1]
        joined = jnp.concatenate(
            [q_part.astype(jnp.bfloat16), k_part.astype(jnp.bfloat16), v_part.astype(jnp.bfloat16)],
            axis=1,
        )
        blocks = [joined[k * block_rows : (k + 1) * block_rows] for k in range(n_row)]
        summed = ring_reduce_scatter(blocks)
        q_sum = summed[:, :q_width]
        key_total_sum = summed[:, q_width : q_width + k_width]
        value_total_sum = summed[:, q_width + k_width :]
        starts = lookup(cache_len, sequences[:seq_dev])
        token_places = (starts[:, None] + jnp.arange(new_len)[None, :]).reshape(-1).astype(jnp.float32)
        row_total = q_sum.shape[0]
        queries = apply_turning(q_sum.reshape(row_total, -1, head_dim), token_places).astype(
            jnp.bfloat16
        )
        rotated_keys = apply_turning(
            key_total_sum.reshape(row_total, -1, head_dim), token_places
        ).astype(jnp.bfloat16)
        values = value_total_sum.reshape(row_total, -1, head_dim).astype(jnp.bfloat16)
        results = jax.vmap(attend)(
            queries.reshape(seq_dev, new_len, -1, head_dim),
            rotated_keys.reshape(seq_dev, new_len, -1, head_dim),
            values.reshape(seq_dev, new_len, -1, head_dim),
            k_cache,
            value_cache,
            starts,
        )
        attended = results.reshape(seq_dev * new_len, -1)
        stacked = ring_all_gather(attended)
        slot_ids = jnp.arange(slot_total, dtype=jnp.int32)
        slot_of = jnp.sum(jnp.where(slot_seq[:, None] == slot_ids[None, :], slot_ids[:, None], 0), axis=0)
        offset = (lookup(position_of, slot_ids // seq_dev) - my_pos) % n_row
        stacked_row_of_slot = lookup(stacked_of_offset, offset) * block_rows + (slot_ids % seq_dev) * new_len
        seq_base = lookup(stacked_row_of_slot, slot_of)
        span = jnp.arange(own_rows, dtype=jnp.int32)
        def half_rows(half):
            t = half * own_rows + span
            return lookup(seq_base, t // new_len) + t % new_len
        theirs_att = jnp.dot(
            one_hot(half_rows(1 - col_index), span_rows), stacked, preferred_element_type=jnp.float32
        ).astype(jnp.bfloat16)
        theirs = jnp.dot(theirs_att, o_weight, preferred_element_type=jnp.float32)
        received = lax.ppermute(theirs.astype(jnp.bfloat16), "col", [(0, 1), (1, 0)])
        mine_att = jnp.dot(
            one_hot(half_rows(col_index), span_rows), stacked, preferred_element_type=jnp.float32
        ).astype(jnp.bfloat16)
        mine = jnp.dot(mine_att, o_weight, preferred_element_type=jnp.float32)
        return (mine + received.astype(jnp.float32)).astype(jnp.bfloat16)

    return body


def solution(mesh):
    return jax.shard_map(
        make_body(row_ring(mesh)),
        mesh=mesh,
        in_specs=(
            P(("groups", "col"), "row"),
            P("row", "col"),
            P("row", "col"),
            P("row", "col"),
            P("col", "row"),
            P(("groups", "row"), None, "col", None),
            P(("groups", "row"), None, "col", None),
            P("groups"),
            P("groups"),
        ),
        out_specs=P(("groups", "col"), "row"),
        check_vma=False,
    )
```

```python
import math

import jax
import jax.numpy as jnp
import numpy as np
from jax import lax
from jax.sharding import PartitionSpec as P

ROPE_BASE = 500000.0


def apply_turning(values, token_places):
    half_dim = values.shape[-1] // 2
    frequency = ROPE_BASE ** (-(2.0 * jnp.arange(half_dim, dtype=jnp.float32)) / values.shape[-1])
    angles = token_places[:, None] * frequency[None, :]
    cosine = jnp.cos(angles)[:, None, :]
    sine_part = jnp.sin(angles)[:, None, :]
    leading = values[..., :half_dim]
    trailing = values[..., half_dim:]
    return jnp.concatenate(
        [leading * cosine - trailing * sine_part, trailing * cosine + leading * sine_part], axis=-1
    )


def attend(queries, incoming_keys, incoming_values, cached_keys, cached_values, length):
    tokens_new, kv_heads, head_dim = incoming_keys.shape
    grouped = queries.reshape(tokens_new, kv_heads, -1, head_dim)
    scale_factor = 1.0 / math.sqrt(head_dim)
    cache_scores = (
        jnp.einsum("nkgd,ckd->kgnc", grouped, cached_keys, preferred_element_type=jnp.float32)
        * scale_factor
    )
    valid_cache = jnp.arange(cached_keys.shape[0]) < length
    cache_scores = jnp.where(valid_cache, cache_scores, -jnp.inf)
    fresh_scores = (
        jnp.einsum("nkgd,mkd->kgnm", grouped, incoming_keys, preferred_element_type=jnp.float32)
        * scale_factor
    )
    causal = jnp.arange(tokens_new)[None, :] <= jnp.arange(tokens_new)[:, None]
    fresh_scores = jnp.where(causal, fresh_scores, -jnp.inf)
    highest = jnp.maximum(jnp.max(cache_scores, axis=-1), jnp.max(fresh_scores, axis=-1))
    cache_weights = jnp.exp(cache_scores - highest[..., None])
    fresh_weights = jnp.exp(fresh_scores - highest[..., None])
    totals = jnp.sum(cache_weights, axis=-1) + jnp.sum(fresh_weights, axis=-1)
    weighted = jnp.einsum(
        "kgnc,ckd->nkgd",
        cache_weights.astype(jnp.bfloat16),
        cached_values,
        preferred_element_type=jnp.float32,
    )
    weighted = weighted + jnp.einsum(
        "kgnm,mkd->nkgd",
        fresh_weights.astype(jnp.bfloat16),
        incoming_values,
        preferred_element_type=jnp.float32,
    )
    normed = weighted / jnp.transpose(totals, (2, 0, 1))[..., None]
    return normed.reshape(tokens_new, -1).astype(jnp.bfloat16)


def row_ring(mesh):
    n_row = mesh.shape["row"]
    natural = list(range(n_row))
    try:
        names = list(mesh.axis_names)
        picked = np.moveaxis(np.asarray(mesh.devices), names.index("row"), 0).reshape(n_row, -1)[:, 0]
        coords = [tuple(d.coords) for d in picked]
    except Exception:
        return natural
    varying = [a for a in range(len(coords[0])) if len({c[a] for c in coords}) > 1]
    if len(varying) != 2:
        return natural
    sizes = {a: len({c[a] for c in coords}) for a in varying}
    inner = [a for a in varying if sizes[a] == 2]
    if not inner or sizes[varying[0]] * sizes[varying[1]] != n_row:
        return natural
    inner = inner[-1]
    outer = [a for a in varying if a != inner][0]
    lo, hi = min(c[inner] for c in coords), max(c[inner] for c in coords)
    first = sorted([i for i in natural if coords[i][inner] == lo], key=lambda i: coords[i][outer])
    second = sorted([i for i in natural if coords[i][inner] == hi], key=lambda i: -coords[i][outer])
    return first + second


def make_body(ring):
    n_row = len(ring)
    position_of = [ring.index(i) for i in range(n_row)]
    forward_hops = n_row // 2
    backward_hops = n_row - 1 - forward_hops
    forward_pairs = [(ring[i], ring[(i + 1) % n_row]) for i in range(n_row)]
    backward_pairs = [(ring[i], ring[(i - 1) % n_row]) for i in range(n_row)]
    gather_offsets = [0]
    for s in range(forward_hops):
        gather_offsets.append(-(s + 1) % n_row)
        if s < backward_hops:
            gather_offsets.append((s + 1) % n_row)
    stacked_of_offset = [gather_offsets.index(d) for d in range(n_row)]

    def tables(seq_dev, new_len):
        slots = np.zeros((n_row, n_row * seq_dev), np.int32)
        stacked_row = np.zeros((n_row, n_row * seq_dev), np.int32)
        for r in range(n_row):
            p = position_of[r]
            for k in range(n_row):
                for j in range(seq_dev):
                    slots[r, k * seq_dev + j] = ring[(p + k) % n_row] * seq_dev + j
            for slot in range(n_row * seq_dev):
                offset = (position_of[slot // seq_dev] - p) % n_row
                stacked_row[r, slot] = (stacked_of_offset[offset] * seq_dev + slot % seq_dev) * new_len
        return slots, stacked_row

    def add_bf16(a, b):
        return (a.astype(jnp.float32) + b.astype(jnp.float32)).astype(jnp.bfloat16)

    def ring_reduce_scatter(blocks):
        if n_row == 1:
            return blocks[0].astype(jnp.float32)
        forward = blocks[forward_hops % n_row]
        backward = blocks[(n_row - backward_hops) % n_row] if backward_hops else None
        got_forward = got_backward = None
        for s in range(forward_hops):
            got_forward = lax.ppermute(forward, "row", forward_pairs)
            if s < backward_hops:
                got_backward = lax.ppermute(backward, "row", backward_pairs)
            if s < forward_hops - 1:
                forward = add_bf16(got_forward, blocks[(forward_hops - s - 1) % n_row])
            if s < backward_hops - 1:
                backward = add_bf16(got_backward, blocks[(s + 1 - backward_hops) % n_row])
        total = got_forward.astype(jnp.float32) + blocks[0].astype(jnp.float32)
        if got_backward is not None:
            total = total + got_backward.astype(jnp.float32)
        return total

    def ring_all_gather(own):
        got = [own]
        forward = backward = own
        for s in range(forward_hops):
            forward = lax.ppermute(forward, "row", forward_pairs)
            got.append(forward)
            if s < backward_hops:
                backward = lax.ppermute(backward, "row", backward_pairs)
                got.append(backward)
        return jnp.concatenate(got, axis=0)

    def lookup(table, index):
        table = jnp.asarray(table, jnp.int32)
        hit = index[..., None] == jnp.arange(table.shape[0], dtype=jnp.int32)
        return jnp.sum(jnp.where(hit, table, 0), axis=-1)

    def one_hot(rows, width):
        return (rows[:, None] == jnp.arange(width, dtype=jnp.int32)[None, :]).astype(jnp.bfloat16)

    def body(
        tokens, q_weight, key_matrix, value_matrix, o_weight, k_cache, value_cache, cache_len, slot_seq
    ):
        row_index = lax.axis_index("row").astype(jnp.int32)
        col_index = lax.axis_index("col").astype(jnp.int32)
        n_col = 2
        seq_dev = k_cache.shape[0]
        head_dim = k_cache.shape[3]
        slot_total = slot_seq.shape[0]
        own_rows = tokens.shape[0]
        span_rows = own_rows * n_col
        new_len = span_rows // slot_total
        block_rows = seq_dev * new_len
        other_tokens = lax.ppermute(tokens, "col", [(0, 1), (1, 0)])
        slots_table, stacked_table = tables(seq_dev, new_len)
        mine_of_row = jnp.arange(n_row, dtype=jnp.int32)[:, None] == row_index
        slots = jnp.sum(jnp.where(mine_of_row, jnp.asarray(slots_table), 0), axis=0)
        sequences = lookup(slot_seq, slots)
        local = jnp.arange(span_rows, dtype=jnp.int32)
        token_rows = jnp.repeat(sequences, new_len) * new_len + local % new_len
        from_own = token_rows // own_rows == col_index
        in_half = token_rows % own_rows
        pick_own = one_hot(jnp.where(from_own, in_half, -1), own_rows)
        pick_other = one_hot(jnp.where(from_own, -1, in_half), own_rows)
        chosen = (
            jnp.dot(pick_own, tokens, preferred_element_type=jnp.float32)
            + jnp.dot(pick_other, other_tokens, preferred_element_type=jnp.float32)
        ).astype(jnp.bfloat16)
        q_part = jnp.dot(chosen, q_weight, preferred_element_type=jnp.float32)
        k_part = jnp.dot(chosen, key_matrix, preferred_element_type=jnp.float32)
        v_part = jnp.dot(chosen, value_matrix, preferred_element_type=jnp.float32)
        q_width = q_part.shape[1]
        k_width = k_part.shape[1]
        joined = jnp.concatenate(
            [q_part.astype(jnp.bfloat16), k_part.astype(jnp.bfloat16), v_part.astype(jnp.bfloat16)],
            axis=1,
        )
        blocks = [joined[k * block_rows : (k + 1) * block_rows] for k in range(n_row)]
        summed = ring_reduce_scatter(blocks)
        summed, late_slot_seq, late_row = lax.optimization_barrier((summed, slot_seq, row_index))
        q_sum = summed[:, :q_width]
        key_total_sum = summed[:, q_width : q_width + k_width]
        value_total_sum = summed[:, q_width + k_width :]
        starts = lookup(cache_len, sequences[:seq_dev])
        token_places = (starts[:, None] + jnp.arange(new_len)[None, :]).reshape(-1).astype(jnp.float32)
        row_total = q_sum.shape[0]
        queries = apply_turning(q_sum.reshape(row_total, -1, head_dim), token_places).astype(
            jnp.bfloat16
        )
        rotated_keys = apply_turning(
            key_total_sum.reshape(row_total, -1, head_dim), token_places
        ).astype(jnp.bfloat16)
        values = value_total_sum.reshape(row_total, -1, head_dim).astype(jnp.bfloat16)
        results = jax.vmap(attend)(
            queries.reshape(seq_dev, new_len, -1, head_dim),
            rotated_keys.reshape(seq_dev, new_len, -1, head_dim),
            values.reshape(seq_dev, new_len, -1, head_dim),
            k_cache,
            value_cache,
            starts,
        )
        attended = results.reshape(seq_dev * new_len, -1)
        stacked = ring_all_gather(attended)
        late_mine = jnp.arange(n_row, dtype=jnp.int32)[:, None] == late_row
        row_of_slot = jnp.sum(jnp.where(late_mine, jnp.asarray(stacked_table), 0), axis=0)
        seq_ids = jnp.arange(slot_total, dtype=jnp.int32)
        seq_base = jnp.sum(
            jnp.where(late_slot_seq[None, :] == seq_ids[:, None], row_of_slot[None, :], 0), axis=1
        )
        half = jnp.where(local < own_rows, 1 - col_index, col_index)
        t = half * own_rows + local % own_rows
        span_order = lookup(seq_base, t // new_len) + t % new_len
        arranged = jnp.dot(
            one_hot(span_order, span_rows), stacked, preferred_element_type=jnp.float32
        ).astype(jnp.bfloat16)
        out_width = o_weight.shape[1]
        n_chunks = 2 if out_width % 256 == 0 else 1
        chunk = out_width // n_chunks
        pieces = []
        for i in range(n_chunks):
            products = jnp.dot(
                arranged, o_weight[:, i * chunk : (i + 1) * chunk], preferred_element_type=jnp.float32
            )
            received = lax.ppermute(
                products[:own_rows].astype(jnp.bfloat16), "col", [(0, 1), (1, 0)]
            )
            pieces.append((products[own_rows:] + received.astype(jnp.float32)).astype(jnp.bfloat16))
        return jnp.concatenate(pieces, axis=1)

    return body


def solution(mesh):
    return jax.shard_map(
        make_body(row_ring(mesh)),
        mesh=mesh,
        in_specs=(
            P(("groups", "col"), "row"),
            P("row", "col"),
            P("row", "col"),
            P("row", "col"),
            P("col", "row"),
            P(("groups", "row"), None, "col", None),
            P(("groups", "row"), None, "col", None),
            P("groups"),
            P("groups"),
        ),
        out_specs=P(("groups", "col"), "row"),
        check_vma=False,
    )
```

```python
import math

import jax
import jax.numpy as jnp
import numpy as np
from jax import lax
from jax.sharding import PartitionSpec as P

ROPE_BASE = 500000.0


def apply_turning(values, token_places):
    half_dim = values.shape[-1] // 2
    frequency = ROPE_BASE ** (-(2.0 * jnp.arange(half_dim, dtype=jnp.float32)) / values.shape[-1])
    angles = token_places[:, None] * frequency[None, :]
    cosine = jnp.cos(angles)[:, None, :]
    sine_part = jnp.sin(angles)[:, None, :]
    leading = values[..., :half_dim]
    trailing = values[..., half_dim:]
    return jnp.concatenate(
        [leading * cosine - trailing * sine_part, trailing * cosine + leading * sine_part], axis=-1
    )


def attend(queries, incoming_keys, incoming_values, cached_keys, cached_values, length):
    tokens_new, kv_heads, head_dim = incoming_keys.shape
    grouped = queries.reshape(tokens_new, kv_heads, -1, head_dim)
    scale_factor = 1.0 / math.sqrt(head_dim)
    cache_scores = (
        jnp.einsum("nkgd,ckd->kgnc", grouped, cached_keys, preferred_element_type=jnp.float32)
        * scale_factor
    )
    valid_cache = jnp.arange(cached_keys.shape[0]) < length
    cache_scores = jnp.where(valid_cache, cache_scores, -jnp.inf)
    fresh_scores = (
        jnp.einsum("nkgd,mkd->kgnm", grouped, incoming_keys, preferred_element_type=jnp.float32)
        * scale_factor
    )
    causal = jnp.arange(tokens_new)[None, :] <= jnp.arange(tokens_new)[:, None]
    fresh_scores = jnp.where(causal, fresh_scores, -jnp.inf)
    highest = jnp.maximum(jnp.max(cache_scores, axis=-1), jnp.max(fresh_scores, axis=-1))
    cache_weights = jnp.exp(cache_scores - highest[..., None])
    fresh_weights = jnp.exp(fresh_scores - highest[..., None])
    totals = jnp.sum(cache_weights, axis=-1) + jnp.sum(fresh_weights, axis=-1)
    weighted = jnp.einsum(
        "kgnc,ckd->nkgd",
        cache_weights.astype(jnp.bfloat16),
        cached_values,
        preferred_element_type=jnp.float32,
    )
    weighted = weighted + jnp.einsum(
        "kgnm,mkd->nkgd",
        fresh_weights.astype(jnp.bfloat16),
        incoming_values,
        preferred_element_type=jnp.float32,
    )
    normed = weighted / jnp.transpose(totals, (2, 0, 1))[..., None]
    return normed.reshape(tokens_new, -1).astype(jnp.bfloat16)


def row_ring(mesh):
    n_row = mesh.shape["row"]
    natural = list(range(n_row))
    try:
        names = list(mesh.axis_names)
        picked = np.moveaxis(np.asarray(mesh.devices), names.index("row"), 0).reshape(n_row, -1)[:, 0]
        coords = [tuple(d.coords) for d in picked]
    except Exception:
        return natural
    varying = [a for a in range(len(coords[0])) if len({c[a] for c in coords}) > 1]
    if len(varying) != 2:
        return natural
    sizes = {a: len({c[a] for c in coords}) for a in varying}
    inner = [a for a in varying if sizes[a] == 2]
    if not inner or sizes[varying[0]] * sizes[varying[1]] != n_row:
        return natural
    inner = inner[-1]
    outer = [a for a in varying if a != inner][0]
    lo, hi = min(c[inner] for c in coords), max(c[inner] for c in coords)
    first = sorted([i for i in natural if coords[i][inner] == lo], key=lambda i: coords[i][outer])
    second = sorted([i for i in natural if coords[i][inner] == hi], key=lambda i: -coords[i][outer])
    return first + second


def make_body(ring):
    n_row = len(ring)
    position_of = [ring.index(i) for i in range(n_row)]
    forward_hops = n_row // 2
    backward_hops = n_row - 1 - forward_hops
    forward_pairs = [(ring[i], ring[(i + 1) % n_row]) for i in range(n_row)]
    backward_pairs = [(ring[i], ring[(i - 1) % n_row]) for i in range(n_row)]
    gather_offsets = [0]
    for s in range(forward_hops):
        gather_offsets.append(-(s + 1) % n_row)
        if s < backward_hops:
            gather_offsets.append((s + 1) % n_row)
    stacked_of_offset = [gather_offsets.index(d) for d in range(n_row)]

    def tables(seq_dev, new_len):
        slots = np.zeros((n_row, n_row * seq_dev), np.int32)
        stacked_row = np.zeros((n_row, n_row * seq_dev), np.int32)
        for r in range(n_row):
            p = position_of[r]
            for k in range(n_row):
                for j in range(seq_dev):
                    slots[r, k * seq_dev + j] = ring[(p + k) % n_row] * seq_dev + j
            for slot in range(n_row * seq_dev):
                offset = (position_of[slot // seq_dev] - p) % n_row
                stacked_row[r, slot] = (stacked_of_offset[offset] * seq_dev + slot % seq_dev) * new_len
        return slots, stacked_row

    def add_bf16(a, b):
        return (a.astype(jnp.float32) + b.astype(jnp.float32)).astype(jnp.bfloat16)

    def ring_reduce_scatter(blocks):
        if n_row == 1:
            return blocks[0].astype(jnp.float32)
        forward = blocks[forward_hops % n_row]
        backward = blocks[(n_row - backward_hops) % n_row] if backward_hops else None
        got_forward = got_backward = None
        for s in range(forward_hops):
            got_forward = lax.ppermute(forward, "row", forward_pairs)
            if s < backward_hops:
                got_backward = lax.ppermute(backward, "row", backward_pairs)
            if s < forward_hops - 1:
                forward = add_bf16(got_forward, blocks[(forward_hops - s - 1) % n_row])
            if s < backward_hops - 1:
                backward = add_bf16(got_backward, blocks[(s + 1 - backward_hops) % n_row])
        total = got_forward.astype(jnp.float32) + blocks[0].astype(jnp.float32)
        if got_backward is not None:
            total = total + got_backward.astype(jnp.float32)
        return total

    def ring_all_gather(own):
        got = [own]
        forward = backward = own
        for s in range(forward_hops):
            forward = lax.ppermute(forward, "row", forward_pairs)
            got.append(forward)
            if s < backward_hops:
                backward = lax.ppermute(backward, "row", backward_pairs)
                got.append(backward)
        return jnp.concatenate(got, axis=0)

    def lookup(table, index):
        table = jnp.asarray(table, jnp.int32)
        hit = index[..., None] == jnp.arange(table.shape[0], dtype=jnp.int32)
        return jnp.sum(jnp.where(hit, table, 0), axis=-1)

    def one_hot(rows, width):
        return (rows[:, None] == jnp.arange(width, dtype=jnp.int32)[None, :]).astype(jnp.bfloat16)

    def body(
        tokens, q_weight, key_matrix, value_matrix, o_weight, k_cache, value_cache, cache_len, slot_seq
    ):
        row_index = lax.axis_index("row").astype(jnp.int32)
        col_index = lax.axis_index("col").astype(jnp.int32)
        n_col = 2
        seq_dev = k_cache.shape[0]
        head_dim = k_cache.shape[3]
        slot_total = slot_seq.shape[0]
        own_rows = tokens.shape[0]
        span_rows = own_rows * n_col
        new_len = span_rows // slot_total
        block_rows = seq_dev * new_len
        other_tokens = lax.ppermute(tokens, "col", [(0, 1), (1, 0)])
        slots_table, stacked_table = tables(seq_dev, new_len)
        mine_of_row = jnp.arange(n_row, dtype=jnp.int32)[:, None] == row_index
        slots = jnp.sum(jnp.where(mine_of_row, jnp.asarray(slots_table), 0), axis=0)
        sequences = lookup(slot_seq, slots)
        local = jnp.arange(span_rows, dtype=jnp.int32)
        token_rows = jnp.repeat(sequences, new_len) * new_len + local % new_len
        from_own = token_rows // own_rows == col_index
        in_half = token_rows % own_rows
        pick_own = one_hot(jnp.where(from_own, in_half, -1), own_rows)
        pick_other = one_hot(jnp.where(from_own, -1, in_half), own_rows)
        chosen = (
            jnp.dot(pick_own, tokens, preferred_element_type=jnp.float32)
            + jnp.dot(pick_other, other_tokens, preferred_element_type=jnp.float32)
        ).astype(jnp.bfloat16)
        n_kv = k_cache.shape[2]
        q_cols = q_weight.shape[1] // n_kv
        k_cols = key_matrix.shape[1] // n_kv
        starts = lookup(cache_len, sequences[:seq_dev])
        token_places = (starts[:, None] + jnp.arange(new_len)[None, :]).reshape(-1).astype(jnp.float32)
        late = None
        arranged_parts = []
        for h in range(n_kv):
            q_part = jnp.dot(
                chosen, q_weight[:, h * q_cols : (h + 1) * q_cols], preferred_element_type=jnp.float32
            )
            k_part = jnp.dot(
                chosen, key_matrix[:, h * k_cols : (h + 1) * k_cols], preferred_element_type=jnp.float32
            )
            v_part = jnp.dot(
                chosen, value_matrix[:, h * k_cols : (h + 1) * k_cols], preferred_element_type=jnp.float32
            )
            joined = jnp.concatenate(
                [q_part.astype(jnp.bfloat16), k_part.astype(jnp.bfloat16), v_part.astype(jnp.bfloat16)],
                axis=1,
            )
            blocks = [joined[k * block_rows : (k + 1) * block_rows] for k in range(n_row)]
            summed = ring_reduce_scatter(blocks)
            if late is None:
                summed, late_slot_seq, late_row = lax.optimization_barrier((summed, slot_seq, row_index))
                late = True
            q_sum = summed[:, :q_cols]
            key_total_sum = summed[:, q_cols : q_cols + k_cols]
            value_total_sum = summed[:, q_cols + k_cols :]
            row_total = q_sum.shape[0]
            queries = apply_turning(q_sum.reshape(row_total, -1, head_dim), token_places).astype(
                jnp.bfloat16
            )
            rotated_keys = apply_turning(
                key_total_sum.reshape(row_total, -1, head_dim), token_places
            ).astype(jnp.bfloat16)
            values = value_total_sum.reshape(row_total, -1, head_dim).astype(jnp.bfloat16)
            results = jax.vmap(attend)(
                queries.reshape(seq_dev, new_len, -1, head_dim),
                rotated_keys.reshape(seq_dev, new_len, -1, head_dim),
                values.reshape(seq_dev, new_len, -1, head_dim),
                k_cache[:, :, h : h + 1, :],
                value_cache[:, :, h : h + 1, :],
                starts,
            )
            attended = results.reshape(seq_dev * new_len, -1)
            arranged_parts.append(ring_all_gather(attended))
        late_mine = jnp.arange(n_row, dtype=jnp.int32)[:, None] == late_row
        row_of_slot = jnp.sum(jnp.where(late_mine, jnp.asarray(stacked_table), 0), axis=0)
        seq_ids = jnp.arange(slot_total, dtype=jnp.int32)
        seq_base = jnp.sum(
            jnp.where(late_slot_seq[None, :] == seq_ids[:, None], row_of_slot[None, :], 0), axis=1
        )
        half = jnp.where(local < own_rows, 1 - col_index, col_index)
        t = half * own_rows + local % own_rows
        span_order = lookup(seq_base, t // new_len) + t % new_len
        order_matrix = one_hot(span_order, span_rows)
        products = None
        for h in range(n_kv):
            arranged = jnp.dot(
                order_matrix, arranged_parts[h], preferred_element_type=jnp.float32
            ).astype(jnp.bfloat16)
            term = jnp.dot(
                arranged, o_weight[h * q_cols : (h + 1) * q_cols], preferred_element_type=jnp.float32
            )
            products = term if products is None else products + term
        received = lax.ppermute(products[:own_rows].astype(jnp.bfloat16), "col", [(0, 1), (1, 0)])
        return (products[own_rows:] + received.astype(jnp.float32)).astype(jnp.bfloat16)

    return body


def solution(mesh):
    return jax.shard_map(
        make_body(row_ring(mesh)),
        mesh=mesh,
        in_specs=(
            P(("groups", "col"), "row"),
            P("row", "col"),
            P("row", "col"),
            P("row", "col"),
            P("col", "row"),
            P(("groups", "row"), None, "col", None),
            P(("groups", "row"), None, "col", None),
            P("groups"),
            P("groups"),
        ),
        out_specs=P(("groups", "col"), "row"),
        check_vma=False,
    )
```

```python
import math

import jax
import jax.numpy as jnp
import numpy as np
from jax import lax
from jax.sharding import PartitionSpec as P

ROPE_BASE = 500000.0


def apply_turning(values, token_places):
    half_dim = values.shape[-1] // 2
    frequency = ROPE_BASE ** (-(2.0 * jnp.arange(half_dim, dtype=jnp.float32)) / values.shape[-1])
    angles = token_places[:, None] * frequency[None, :]
    cosine = jnp.cos(angles)[:, None, :]
    sine_part = jnp.sin(angles)[:, None, :]
    leading = values[..., :half_dim]
    trailing = values[..., half_dim:]
    return jnp.concatenate(
        [leading * cosine - trailing * sine_part, trailing * cosine + leading * sine_part], axis=-1
    )


def attend(queries, incoming_keys, incoming_values, cached_keys, cached_values, length):
    tokens_new, kv_heads, head_dim = incoming_keys.shape
    grouped = queries.reshape(tokens_new, kv_heads, -1, head_dim)
    scale_factor = 1.0 / math.sqrt(head_dim)
    cache_scores = (
        jnp.einsum("nkgd,ckd->kgnc", grouped, cached_keys, preferred_element_type=jnp.float32)
        * scale_factor
    )
    valid_cache = jnp.arange(cached_keys.shape[0]) < length
    cache_scores = jnp.where(valid_cache, cache_scores, -jnp.inf)
    fresh_scores = (
        jnp.einsum("nkgd,mkd->kgnm", grouped, incoming_keys, preferred_element_type=jnp.float32)
        * scale_factor
    )
    causal = jnp.arange(tokens_new)[None, :] <= jnp.arange(tokens_new)[:, None]
    fresh_scores = jnp.where(causal, fresh_scores, -jnp.inf)
    highest = jnp.maximum(jnp.max(cache_scores, axis=-1), jnp.max(fresh_scores, axis=-1))
    cache_weights = jnp.exp(cache_scores - highest[..., None])
    fresh_weights = jnp.exp(fresh_scores - highest[..., None])
    totals = jnp.sum(cache_weights, axis=-1) + jnp.sum(fresh_weights, axis=-1)
    weighted = jnp.einsum(
        "kgnc,ckd->nkgd",
        cache_weights.astype(jnp.bfloat16),
        cached_values,
        preferred_element_type=jnp.float32,
    )
    weighted = weighted + jnp.einsum(
        "kgnm,mkd->nkgd",
        fresh_weights.astype(jnp.bfloat16),
        incoming_values,
        preferred_element_type=jnp.float32,
    )
    normed = weighted / jnp.transpose(totals, (2, 0, 1))[..., None]
    return normed.reshape(tokens_new, -1).astype(jnp.bfloat16)


def row_ring(mesh):
    n_row = mesh.shape["row"]
    natural = list(range(n_row))
    try:
        names = list(mesh.axis_names)
        picked = np.moveaxis(np.asarray(mesh.devices), names.index("row"), 0).reshape(n_row, -1)[:, 0]
        coords = [tuple(d.coords) for d in picked]
    except Exception:
        return natural
    varying = [a for a in range(len(coords[0])) if len({c[a] for c in coords}) > 1]
    if len(varying) != 2:
        return natural
    sizes = {a: len({c[a] for c in coords}) for a in varying}
    inner = [a for a in varying if sizes[a] == 2]
    if not inner or sizes[varying[0]] * sizes[varying[1]] != n_row:
        return natural
    inner = inner[-1]
    outer = [a for a in varying if a != inner][0]
    lo, hi = min(c[inner] for c in coords), max(c[inner] for c in coords)
    first = sorted([i for i in natural if coords[i][inner] == lo], key=lambda i: coords[i][outer])
    second = sorted([i for i in natural if coords[i][inner] == hi], key=lambda i: -coords[i][outer])
    return first + second


def make_body(ring):
    n_row = len(ring)
    position_of = [ring.index(i) for i in range(n_row)]
    forward_hops = n_row // 2
    backward_hops = n_row - 1 - forward_hops
    forward_pairs = [(ring[i], ring[(i + 1) % n_row]) for i in range(n_row)]
    backward_pairs = [(ring[i], ring[(i - 1) % n_row]) for i in range(n_row)]
    gather_offsets = [0]
    for s in range(forward_hops):
        gather_offsets.append(-(s + 1) % n_row)
        if s < backward_hops:
            gather_offsets.append((s + 1) % n_row)
    stacked_of_offset = [gather_offsets.index(d) for d in range(n_row)]

    def tables(seq_dev, new_len):
        slots = np.zeros((n_row, n_row * seq_dev), np.int32)
        stacked_row = np.zeros((n_row, n_row * seq_dev), np.int32)
        for r in range(n_row):
            p = position_of[r]
            for k in range(n_row):
                for j in range(seq_dev):
                    slots[r, k * seq_dev + j] = ring[(p + k) % n_row] * seq_dev + j
            for slot in range(n_row * seq_dev):
                offset = (position_of[slot // seq_dev] - p) % n_row
                stacked_row[r, slot] = (stacked_of_offset[offset] * seq_dev + slot % seq_dev) * new_len
        return slots, stacked_row

    def add_bf16(a, b):
        return (a.astype(jnp.float32) + b.astype(jnp.float32)).astype(jnp.bfloat16)

    def ring_reduce_scatter(blocks):
        if n_row == 1:
            return blocks[0].astype(jnp.float32)
        forward = blocks[forward_hops % n_row]
        backward = blocks[(n_row - backward_hops) % n_row] if backward_hops else None
        got_forward = got_backward = None
        for s in range(forward_hops):
            got_forward = lax.ppermute(forward, "row", forward_pairs)
            if s < backward_hops:
                got_backward = lax.ppermute(backward, "row", backward_pairs)
            if s < forward_hops - 1:
                forward = add_bf16(got_forward, blocks[(forward_hops - s - 1) % n_row])
            if s < backward_hops - 1:
                backward = add_bf16(got_backward, blocks[(s + 1 - backward_hops) % n_row])
        total = got_forward.astype(jnp.float32) + blocks[0].astype(jnp.float32)
        if got_backward is not None:
            total = total + got_backward.astype(jnp.float32)
        return total

    def ring_all_gather(own):
        got = [own]
        forward = backward = own
        for s in range(forward_hops):
            forward = lax.ppermute(forward, "row", forward_pairs)
            got.append(forward)
            if s < backward_hops:
                backward = lax.ppermute(backward, "row", backward_pairs)
                got.append(backward)
        return jnp.concatenate(got, axis=0)

    def lookup(table, index):
        table = jnp.asarray(table, jnp.int32)
        hit = index[..., None] == jnp.arange(table.shape[0], dtype=jnp.int32)
        return jnp.sum(jnp.where(hit, table, 0), axis=-1)

    def one_hot(rows, width):
        return (rows[:, None] == jnp.arange(width, dtype=jnp.int32)[None, :]).astype(jnp.bfloat16)

    def body(
        tokens, q_weight, key_matrix, value_matrix, o_weight, k_cache, value_cache, cache_len, slot_seq
    ):
        row_index = lax.axis_index("row").astype(jnp.int32)
        col_index = lax.axis_index("col").astype(jnp.int32)
        n_col = 2
        seq_dev = k_cache.shape[0]
        head_dim = k_cache.shape[3]
        slot_total = slot_seq.shape[0]
        own_rows = tokens.shape[0]
        span_rows = own_rows * n_col
        new_len = span_rows // slot_total
        block_rows = seq_dev * new_len
        other_tokens = lax.ppermute(tokens, "col", [(0, 1), (1, 0)])
        slots_table, stacked_table = tables(seq_dev, new_len)
        mine_of_row = jnp.arange(n_row, dtype=jnp.int32)[:, None] == row_index
        slots = jnp.sum(jnp.where(mine_of_row, jnp.asarray(slots_table), 0), axis=0)
        sequences = lookup(slot_seq, slots)
        local = jnp.arange(span_rows, dtype=jnp.int32)
        token_rows = jnp.repeat(sequences, new_len) * new_len + local % new_len
        from_own = token_rows // own_rows == col_index
        in_half = token_rows % own_rows
        pick_own = one_hot(jnp.where(from_own, in_half, -1), own_rows)
        pick_other = one_hot(jnp.where(from_own, -1, in_half), own_rows)
        chosen = (
            jnp.dot(pick_own, tokens, preferred_element_type=jnp.float32)
            + jnp.dot(pick_other, other_tokens, preferred_element_type=jnp.float32)
        ).astype(jnp.bfloat16)
        n_kv = k_cache.shape[2]
        q_cols = q_weight.shape[1] // n_kv
        k_cols = key_matrix.shape[1] // n_kv
        k_part = jnp.dot(chosen, key_matrix, preferred_element_type=jnp.float32).astype(jnp.bfloat16)
        v_part = jnp.dot(chosen, value_matrix, preferred_element_type=jnp.float32).astype(jnp.bfloat16)
        q_sums, k_sums, v_sums = [], [], []
        for h in range(n_kv):
            q_part = jnp.dot(
                chosen, q_weight[:, h * q_cols : (h + 1) * q_cols], preferred_element_type=jnp.float32
            ).astype(jnp.bfloat16)
            joined = jnp.concatenate(
                [q_part, k_part[:, h * k_cols : (h + 1) * k_cols], v_part[:, h * k_cols : (h + 1) * k_cols]],
                axis=1,
            )
            blocks = [joined[k * block_rows : (k + 1) * block_rows] for k in range(n_row)]
            summed = ring_reduce_scatter(blocks)
            q_sums.append(summed[:, :q_cols])
            k_sums.append(summed[:, q_cols : q_cols + k_cols])
            v_sums.append(summed[:, q_cols + k_cols :])
        q_sum = jnp.concatenate(q_sums, axis=1)
        key_total_sum = jnp.concatenate(k_sums, axis=1)
        value_total_sum = jnp.concatenate(v_sums, axis=1)
        q_sum, late_slot_seq, late_row = lax.optimization_barrier((q_sum, slot_seq, row_index))
        starts = lookup(cache_len, sequences[:seq_dev])
        token_places = (starts[:, None] + jnp.arange(new_len)[None, :]).reshape(-1).astype(jnp.float32)
        row_total = q_sum.shape[0]
        queries = apply_turning(q_sum.reshape(row_total, -1, head_dim), token_places).astype(
            jnp.bfloat16
        )
        rotated_keys = apply_turning(
            key_total_sum.reshape(row_total, -1, head_dim), token_places
        ).astype(jnp.bfloat16)
        values = value_total_sum.reshape(row_total, -1, head_dim).astype(jnp.bfloat16)
        results = jax.vmap(attend)(
            queries.reshape(seq_dev, new_len, -1, head_dim),
            rotated_keys.reshape(seq_dev, new_len, -1, head_dim),
            values.reshape(seq_dev, new_len, -1, head_dim),
            k_cache,
            value_cache,
            starts,
        )
        attended = results.reshape(seq_dev * new_len, -1)
        stacked = jnp.concatenate(
            [ring_all_gather(attended[:, h * q_cols : (h + 1) * q_cols]) for h in range(n_kv)], axis=1
        )
        late_mine = jnp.arange(n_row, dtype=jnp.int32)[:, None] == late_row
        row_of_slot = jnp.sum(jnp.where(late_mine, jnp.asarray(stacked_table), 0), axis=0)
        seq_ids = jnp.arange(slot_total, dtype=jnp.int32)
        seq_base = jnp.sum(
            jnp.where(late_slot_seq[None, :] == seq_ids[:, None], row_of_slot[None, :], 0), axis=1
        )
        half = jnp.where(local < own_rows, 1 - col_index, col_index)
        t = half * own_rows + local % own_rows
        span_order = lookup(seq_base, t // new_len) + t % new_len
        arranged = jnp.dot(
            one_hot(span_order, span_rows), stacked, preferred_element_type=jnp.float32
        ).astype(jnp.bfloat16)
        arranged = lax.optimization_barrier(arranged)
        products = jnp.dot(arranged, o_weight, preferred_element_type=jnp.float32)
        received = lax.ppermute(products[:own_rows].astype(jnp.bfloat16), "col", [(0, 1), (1, 0)])
        return (products[own_rows:] + received.astype(jnp.float32)).astype(jnp.bfloat16)

    return body


def solution(mesh):
    return jax.shard_map(
        make_body(row_ring(mesh)),
        mesh=mesh,
        in_specs=(
            P(("groups", "col"), "row"),
            P("row", "col"),
            P("row", "col"),
            P("row", "col"),
            P("col", "row"),
            P(("groups", "row"), None, "col", None),
            P(("groups", "row"), None, "col", None),
            P("groups"),
            P("groups"),
        ),
        out_specs=P(("groups", "col"), "row"),
        check_vma=False,
    )
```

```python
import math

import jax
import jax.numpy as jnp
import numpy as np
from jax import lax
from jax.sharding import PartitionSpec as P

ROPE_BASE = 500000.0


def apply_turning(values, token_places):
    half_dim = values.shape[-1] // 2
    frequency = ROPE_BASE ** (-(2.0 * jnp.arange(half_dim, dtype=jnp.float32)) / values.shape[-1])
    angles = token_places[:, None] * frequency[None, :]
    cosine = jnp.cos(angles)[:, None, :]
    sine_part = jnp.sin(angles)[:, None, :]
    leading = values[..., :half_dim]
    trailing = values[..., half_dim:]
    return jnp.concatenate(
        [leading * cosine - trailing * sine_part, trailing * cosine + leading * sine_part], axis=-1
    )


def attend(queries, incoming_keys, incoming_values, cached_keys, cached_values, length):
    tokens_new, kv_heads, head_dim = incoming_keys.shape
    grouped = queries.reshape(tokens_new, kv_heads, -1, head_dim)
    scale_factor = 1.0 / math.sqrt(head_dim)
    cache_scores = (
        jnp.einsum("nkgd,ckd->kgnc", grouped, cached_keys, preferred_element_type=jnp.float32)
        * scale_factor
    )
    valid_cache = jnp.arange(cached_keys.shape[0]) < length
    cache_scores = jnp.where(valid_cache, cache_scores, -jnp.inf)
    fresh_scores = (
        jnp.einsum("nkgd,mkd->kgnm", grouped, incoming_keys, preferred_element_type=jnp.float32)
        * scale_factor
    )
    causal = jnp.arange(tokens_new)[None, :] <= jnp.arange(tokens_new)[:, None]
    fresh_scores = jnp.where(causal, fresh_scores, -jnp.inf)
    highest = jnp.maximum(jnp.max(cache_scores, axis=-1), jnp.max(fresh_scores, axis=-1))
    cache_weights = jnp.exp(cache_scores - highest[..., None])
    fresh_weights = jnp.exp(fresh_scores - highest[..., None])
    totals = jnp.sum(cache_weights, axis=-1) + jnp.sum(fresh_weights, axis=-1)
    weighted = jnp.einsum(
        "kgnc,ckd->nkgd",
        cache_weights.astype(jnp.bfloat16),
        cached_values,
        preferred_element_type=jnp.float32,
    )
    weighted = weighted + jnp.einsum(
        "kgnm,mkd->nkgd",
        fresh_weights.astype(jnp.bfloat16),
        incoming_values,
        preferred_element_type=jnp.float32,
    )
    normed = weighted / jnp.transpose(totals, (2, 0, 1))[..., None]
    return normed.reshape(tokens_new, -1).astype(jnp.bfloat16)


def row_ring(mesh):
    n_row = mesh.shape["row"]
    natural = list(range(n_row))
    try:
        names = list(mesh.axis_names)
        picked = np.moveaxis(np.asarray(mesh.devices), names.index("row"), 0).reshape(n_row, -1)[:, 0]
        coords = [tuple(d.coords) for d in picked]
    except Exception:
        return natural
    varying = [a for a in range(len(coords[0])) if len({c[a] for c in coords}) > 1]
    if len(varying) != 2:
        return natural
    sizes = {a: len({c[a] for c in coords}) for a in varying}
    inner = [a for a in varying if sizes[a] == 2]
    if not inner or sizes[varying[0]] * sizes[varying[1]] != n_row:
        return natural
    inner = inner[-1]
    outer = [a for a in varying if a != inner][0]
    lo, hi = min(c[inner] for c in coords), max(c[inner] for c in coords)
    first = sorted([i for i in natural if coords[i][inner] == lo], key=lambda i: coords[i][outer])
    second = sorted([i for i in natural if coords[i][inner] == hi], key=lambda i: -coords[i][outer])
    return first + second


def make_body(ring):
    n_row = len(ring)
    position_of = [ring.index(i) for i in range(n_row)]
    forward_hops = n_row // 2
    backward_hops = n_row - 1 - forward_hops
    forward_pairs = [(ring[i], ring[(i + 1) % n_row]) for i in range(n_row)]
    backward_pairs = [(ring[i], ring[(i - 1) % n_row]) for i in range(n_row)]
    balanced = n_row % 2 == 0
    if balanced:
        forward_hops = backward_hops = n_row // 2
    gather_offsets = [0]
    full_forward = forward_hops - 1 if balanced else forward_hops
    full_backward = backward_hops - 1 if balanced else backward_hops
    for s in range(max(full_forward, full_backward)):
        if s < full_forward:
            gather_offsets.append(-(s + 1) % n_row)
        if s < full_backward:
            gather_offsets.append((s + 1) % n_row)
    if balanced and n_row > 1:
        gather_offsets.append(n_row // 2)
    stacked_of_offset = [gather_offsets.index(d) for d in range(n_row)]

    def tables(seq_dev, new_len):
        slots = np.zeros((n_row, n_row * seq_dev), np.int32)
        stacked_row = np.zeros((n_row, n_row * seq_dev), np.int32)
        for r in range(n_row):
            p = position_of[r]
            for k in range(n_row):
                for j in range(seq_dev):
                    slots[r, k * seq_dev + j] = ring[(p + k) % n_row] * seq_dev + j
            for slot in range(n_row * seq_dev):
                offset = (position_of[slot // seq_dev] - p) % n_row
                stacked_row[r, slot] = (stacked_of_offset[offset] * seq_dev + slot % seq_dev) * new_len
        return slots, stacked_row

    def add_bf16(a, b):
        return (a.astype(jnp.float32) + b.astype(jnp.float32)).astype(jnp.bfloat16)

    def ring_reduce_scatter(blocks):
        if n_row == 1:
            return blocks[0].astype(jnp.float32)
        width = blocks[0].shape[1]
        split = width // 2
        if balanced:
            forward = blocks[forward_hops][:, :split]
            backward = blocks[forward_hops][:, split:]
        else:
            forward = blocks[forward_hops % n_row]
            backward = blocks[(n_row - backward_hops) % n_row] if backward_hops else None
        got_forward = got_backward = None
        for s in range(max(forward_hops, backward_hops)):
            if s < forward_hops:
                got_forward = lax.ppermute(forward, "row", forward_pairs)
            if s < backward_hops:
                got_backward = lax.ppermute(backward, "row", backward_pairs)
            if s < forward_hops - 1:
                own = blocks[(forward_hops - s - 1) % n_row]
                if balanced and s == 0:
                    forward = jnp.concatenate([add_bf16(got_forward, own[:, :split]), own[:, split:]], axis=1)
                else:
                    forward = add_bf16(got_forward, own)
            if s < backward_hops - 1:
                own = blocks[(s + 1 - backward_hops) % n_row]
                if balanced and s == 0:
                    backward = jnp.concatenate([own[:, :split], add_bf16(got_backward, own[:, split:])], axis=1)
                else:
                    backward = add_bf16(got_backward, own)
        total = blocks[0].astype(jnp.float32)
        if balanced and forward_hops == 1:
            return total + jnp.concatenate([got_forward, got_backward], axis=1).astype(jnp.float32)
        total = total + got_forward.astype(jnp.float32)
        if got_backward is not None:
            total = total + got_backward.astype(jnp.float32)
        return total

    def ring_all_gather(own):
        if n_row == 1:
            return own
        split = own.shape[1] // 2
        got = [own]
        forward = backward = own
        for s in range(max(full_forward, full_backward)):
            if s < full_forward:
                forward = lax.ppermute(forward, "row", forward_pairs)
                got.append(forward)
            if s < full_backward:
                backward = lax.ppermute(backward, "row", backward_pairs)
                got.append(backward)
        if balanced:
            first = lax.ppermute(forward[:, :split], "row", forward_pairs)
            second = lax.ppermute(backward[:, split:], "row", backward_pairs)
            got.append(jnp.concatenate([first, second], axis=1))
        return jnp.concatenate(got, axis=0)

    def lookup(table, index):
        table = jnp.asarray(table, jnp.int32)
        hit = index[..., None] == jnp.arange(table.shape[0], dtype=jnp.int32)
        return jnp.sum(jnp.where(hit, table, 0), axis=-1)

    def one_hot(rows, width):
        return (rows[:, None] == jnp.arange(width, dtype=jnp.int32)[None, :]).astype(jnp.bfloat16)

    def body(
        tokens, q_weight, key_matrix, value_matrix, o_weight, k_cache, value_cache, cache_len, slot_seq
    ):
        row_index = lax.axis_index("row").astype(jnp.int32)
        col_index = lax.axis_index("col").astype(jnp.int32)
        n_col = 2
        seq_dev = k_cache.shape[0]
        head_dim = k_cache.shape[3]
        slot_total = slot_seq.shape[0]
        own_rows = tokens.shape[0]
        span_rows = own_rows * n_col
        new_len = span_rows // slot_total
        block_rows = seq_dev * new_len
        other_tokens = lax.ppermute(tokens, "col", [(0, 1), (1, 0)])
        slots_table, stacked_table = tables(seq_dev, new_len)
        mine_of_row = jnp.arange(n_row, dtype=jnp.int32)[:, None] == row_index
        slots = jnp.sum(jnp.where(mine_of_row, jnp.asarray(slots_table), 0), axis=0)
        sequences = lookup(slot_seq, slots)
        local = jnp.arange(span_rows, dtype=jnp.int32)
        token_rows = jnp.repeat(sequences, new_len) * new_len + local % new_len
        from_own = token_rows // own_rows == col_index
        in_half = token_rows % own_rows
        pick_own = one_hot(jnp.where(from_own, in_half, -1), own_rows)
        pick_other = one_hot(jnp.where(from_own, -1, in_half), own_rows)
        chosen = (
            jnp.dot(pick_own, tokens, preferred_element_type=jnp.float32)
            + jnp.dot(pick_other, other_tokens, preferred_element_type=jnp.float32)
        ).astype(jnp.bfloat16)
        n_kv = k_cache.shape[2]
        q_cols = q_weight.shape[1] // n_kv
        k_cols = key_matrix.shape[1] // n_kv
        k_part = jnp.dot(chosen, key_matrix, preferred_element_type=jnp.float32).astype(jnp.bfloat16)
        v_part = jnp.dot(chosen, value_matrix, preferred_element_type=jnp.float32).astype(jnp.bfloat16)
        q_sums, k_sums, v_sums = [], [], []
        for h in range(n_kv):
            q_part = jnp.dot(
                chosen, q_weight[:, h * q_cols : (h + 1) * q_cols], preferred_element_type=jnp.float32
            ).astype(jnp.bfloat16)
            joined = jnp.concatenate(
                [q_part, k_part[:, h * k_cols : (h + 1) * k_cols], v_part[:, h * k_cols : (h + 1) * k_cols]],
                axis=1,
            )
            blocks = [joined[k * block_rows : (k + 1) * block_rows] for k in range(n_row)]
            summed = ring_reduce_scatter(blocks)
            q_sums.append(summed[:, :q_cols])
            k_sums.append(summed[:, q_cols : q_cols + k_cols])
            v_sums.append(summed[:, q_cols + k_cols :])
        q_sum = jnp.concatenate(q_sums, axis=1)
        key_total_sum = jnp.concatenate(k_sums, axis=1)
        value_total_sum = jnp.concatenate(v_sums, axis=1)
        q_sum, late_slot_seq, late_row = lax.optimization_barrier((q_sum, slot_seq, row_index))
        starts = lookup(cache_len, sequences[:seq_dev])
        token_places = (starts[:, None] + jnp.arange(new_len)[None, :]).reshape(-1).astype(jnp.float32)
        row_total = q_sum.shape[0]
        queries = apply_turning(q_sum.reshape(row_total, -1, head_dim), token_places).astype(
            jnp.bfloat16
        )
        rotated_keys = apply_turning(
            key_total_sum.reshape(row_total, -1, head_dim), token_places
        ).astype(jnp.bfloat16)
        values = value_total_sum.reshape(row_total, -1, head_dim).astype(jnp.bfloat16)
        results = jax.vmap(attend)(
            queries.reshape(seq_dev, new_len, -1, head_dim),
            rotated_keys.reshape(seq_dev, new_len, -1, head_dim),
            values.reshape(seq_dev, new_len, -1, head_dim),
            k_cache,
            value_cache,
            starts,
        )
        attended = results.reshape(seq_dev * new_len, -1)
        stacked = jnp.concatenate(
            [ring_all_gather(attended[:, h * q_cols : (h + 1) * q_cols]) for h in range(n_kv)], axis=1
        )
        late_mine = jnp.arange(n_row, dtype=jnp.int32)[:, None] == late_row
        row_of_slot = jnp.sum(jnp.where(late_mine, jnp.asarray(stacked_table), 0), axis=0)
        seq_ids = jnp.arange(slot_total, dtype=jnp.int32)
        seq_base = jnp.sum(
            jnp.where(late_slot_seq[None, :] == seq_ids[:, None], row_of_slot[None, :], 0), axis=1
        )
        half = jnp.where(local < own_rows, 1 - col_index, col_index)
        t = half * own_rows + local % own_rows
        span_order = lookup(seq_base, t // new_len) + t % new_len
        arranged = jnp.dot(
            one_hot(span_order, span_rows), stacked, preferred_element_type=jnp.float32
        ).astype(jnp.bfloat16)
        arranged = lax.optimization_barrier(arranged)
        products = jnp.dot(arranged, o_weight, preferred_element_type=jnp.float32)
        received = lax.ppermute(products[:own_rows].astype(jnp.bfloat16), "col", [(0, 1), (1, 0)])
        return (products[own_rows:] + received.astype(jnp.float32)).astype(jnp.bfloat16)

    return body


def solution(mesh):
    return jax.shard_map(
        make_body(row_ring(mesh)),
        mesh=mesh,
        in_specs=(
            P(("groups", "col"), "row"),
            P("row", "col"),
            P("row", "col"),
            P("row", "col"),
            P("col", "row"),
            P(("groups", "row"), None, "col", None),
            P(("groups", "row"), None, "col", None),
            P("groups"),
            P("groups"),
        ),
        out_specs=P(("groups", "col"), "row"),
        check_vma=False,
    )
```

```python
import math

import jax
import jax.numpy as jnp
import numpy as np
from jax import lax
from jax.sharding import PartitionSpec as P

ROPE_BASE = 500000.0


def apply_turning(values, token_places):
    half_dim = values.shape[-1] // 2
    frequency = ROPE_BASE ** (-(2.0 * jnp.arange(half_dim, dtype=jnp.float32)) / values.shape[-1])
    angles = token_places[:, None] * frequency[None, :]
    cosine = jnp.cos(angles)[:, None, :]
    sine_part = jnp.sin(angles)[:, None, :]
    leading = values[..., :half_dim]
    trailing = values[..., half_dim:]
    return jnp.concatenate(
        [leading * cosine - trailing * sine_part, trailing * cosine + leading * sine_part], axis=-1
    )


def attend(queries, incoming_keys, incoming_values, cached_keys, cached_values, length):
    tokens_new, kv_heads, head_dim = incoming_keys.shape
    grouped = queries.reshape(tokens_new, kv_heads, -1, head_dim)
    scale_factor = 1.0 / math.sqrt(head_dim)
    cache_scores = (
        jnp.einsum("nkgd,ckd->kgnc", grouped, cached_keys, preferred_element_type=jnp.float32)
        * scale_factor
    )
    valid_cache = jnp.arange(cached_keys.shape[0]) < length
    cache_scores = jnp.where(valid_cache, cache_scores, -jnp.inf)
    fresh_scores = (
        jnp.einsum("nkgd,mkd->kgnm", grouped, incoming_keys, preferred_element_type=jnp.float32)
        * scale_factor
    )
    causal = jnp.arange(tokens_new)[None, :] <= jnp.arange(tokens_new)[:, None]
    fresh_scores = jnp.where(causal, fresh_scores, -jnp.inf)
    highest = jnp.maximum(jnp.max(cache_scores, axis=-1), jnp.max(fresh_scores, axis=-1))
    cache_weights = jnp.exp(cache_scores - highest[..., None])
    fresh_weights = jnp.exp(fresh_scores - highest[..., None])
    totals = jnp.sum(cache_weights, axis=-1) + jnp.sum(fresh_weights, axis=-1)
    weighted = jnp.einsum(
        "kgnc,ckd->nkgd",
        cache_weights.astype(jnp.bfloat16),
        cached_values,
        preferred_element_type=jnp.float32,
    )
    weighted = weighted + jnp.einsum(
        "kgnm,mkd->nkgd",
        fresh_weights.astype(jnp.bfloat16),
        incoming_values,
        preferred_element_type=jnp.float32,
    )
    normed = weighted / jnp.transpose(totals, (2, 0, 1))[..., None]
    return normed.reshape(tokens_new, -1).astype(jnp.bfloat16)


def row_ring(mesh):
    n_row = mesh.shape["row"]
    natural = list(range(n_row))
    try:
        names = list(mesh.axis_names)
        picked = np.moveaxis(np.asarray(mesh.devices), names.index("row"), 0).reshape(n_row, -1)[:, 0]
        coords = [tuple(d.coords) for d in picked]
    except Exception:
        return natural
    varying = [a for a in range(len(coords[0])) if len({c[a] for c in coords}) > 1]
    if len(varying) != 2:
        return natural
    sizes = {a: len({c[a] for c in coords}) for a in varying}
    inner = [a for a in varying if sizes[a] == 2]
    if not inner or sizes[varying[0]] * sizes[varying[1]] != n_row:
        return natural
    inner = inner[-1]
    outer = [a for a in varying if a != inner][0]
    lo, hi = min(c[inner] for c in coords), max(c[inner] for c in coords)
    first = sorted([i for i in natural if coords[i][inner] == lo], key=lambda i: coords[i][outer])
    second = sorted([i for i in natural if coords[i][inner] == hi], key=lambda i: -coords[i][outer])
    return first + second


def make_body(ring):
    n_row = len(ring)
    position_of = [ring.index(i) for i in range(n_row)]
    forward_hops = n_row // 2
    backward_hops = n_row - 1 - forward_hops
    forward_pairs = [(ring[i], ring[(i + 1) % n_row]) for i in range(n_row)]
    backward_pairs = [(ring[i], ring[(i - 1) % n_row]) for i in range(n_row)]
    gather_offsets = [0]
    for s in range(forward_hops):
        gather_offsets.append(-(s + 1) % n_row)
        if s < backward_hops:
            gather_offsets.append((s + 1) % n_row)
    stacked_of_offset = [gather_offsets.index(d) for d in range(n_row)]

    def tables(seq_dev, new_len):
        slots = np.zeros((n_row, n_row * seq_dev), np.int32)
        stacked_row = np.zeros((n_row, n_row * seq_dev), np.int32)
        for r in range(n_row):
            p = position_of[r]
            for k in range(n_row):
                for j in range(seq_dev):
                    slots[r, k * seq_dev + j] = ring[(p + k) % n_row] * seq_dev + j
            for slot in range(n_row * seq_dev):
                offset = (position_of[slot // seq_dev] - p) % n_row
                stacked_row[r, slot] = (stacked_of_offset[offset] * seq_dev + slot % seq_dev) * new_len
        return slots, stacked_row

    def add_bf16(a, b):
        return (a.astype(jnp.float32) + b.astype(jnp.float32)).astype(jnp.bfloat16)

    def ring_reduce_scatter(blocks):
        if n_row == 1:
            return blocks[0].astype(jnp.float32)
        forward = blocks[forward_hops % n_row]
        backward = blocks[(n_row - backward_hops) % n_row] if backward_hops else None
        got_forward = got_backward = None
        for s in range(forward_hops):
            got_forward = lax.ppermute(forward, "row", forward_pairs)
            if s < backward_hops:
                got_backward = lax.ppermute(backward, "row", backward_pairs)
            if s < forward_hops - 1:
                forward = add_bf16(got_forward, blocks[(forward_hops - s - 1) % n_row])
            if s < backward_hops - 1:
                backward = add_bf16(got_backward, blocks[(s + 1 - backward_hops) % n_row])
        total = got_forward.astype(jnp.float32) + blocks[0].astype(jnp.float32)
        if got_backward is not None:
            total = total + got_backward.astype(jnp.float32)
        return total

    def ring_all_gather(own):
        got = [own]
        forward = backward = own
        for s in range(forward_hops):
            forward = lax.ppermute(forward, "row", forward_pairs)
            got.append(forward)
            if s < backward_hops:
                backward = lax.ppermute(backward, "row", backward_pairs)
                got.append(backward)
        return jnp.concatenate(got, axis=0)

    def lookup(table, index):
        table = jnp.asarray(table, jnp.int32)
        hit = index[..., None] == jnp.arange(table.shape[0], dtype=jnp.int32)
        return jnp.sum(jnp.where(hit, table, 0), axis=-1)

    def one_hot(rows, width):
        return (rows[:, None] == jnp.arange(width, dtype=jnp.int32)[None, :]).astype(jnp.bfloat16)

    def body(
        tokens, q_weight, key_matrix, value_matrix, o_weight, k_cache, value_cache, cache_len, slot_seq
    ):
        row_index = lax.axis_index("row").astype(jnp.int32)
        col_index = lax.axis_index("col").astype(jnp.int32)
        n_col = 2
        seq_dev = k_cache.shape[0]
        head_dim = k_cache.shape[3]
        slot_total = slot_seq.shape[0]
        own_rows = tokens.shape[0]
        span_rows = own_rows * n_col
        new_len = span_rows // slot_total
        block_rows = seq_dev * new_len
        other_tokens = lax.ppermute(tokens, "col", [(0, 1), (1, 0)])
        slots_table, stacked_table = tables(seq_dev, new_len)
        mine_of_row = jnp.arange(n_row, dtype=jnp.int32)[:, None] == row_index
        slots = jnp.sum(jnp.where(mine_of_row, jnp.asarray(slots_table), 0), axis=0)
        sequences = lookup(slot_seq, slots)
        local = jnp.arange(span_rows, dtype=jnp.int32)
        token_rows = jnp.repeat(sequences, new_len) * new_len + local % new_len
        from_own = token_rows // own_rows == col_index
        in_half = token_rows % own_rows
        pick_own = one_hot(jnp.where(from_own, in_half, -1), own_rows)
        pick_other = one_hot(jnp.where(from_own, -1, in_half), own_rows)
        chosen = (
            jnp.dot(pick_own, tokens, preferred_element_type=jnp.float32)
            + jnp.dot(pick_other, other_tokens, preferred_element_type=jnp.float32)
        ).astype(jnp.bfloat16)
        n_kv = k_cache.shape[2]
        q_cols = q_weight.shape[1] // n_kv
        k_cols = key_matrix.shape[1] // n_kv
        k_part = jnp.dot(chosen, key_matrix, preferred_element_type=jnp.float32).astype(jnp.bfloat16)
        v_part = jnp.dot(chosen, value_matrix, preferred_element_type=jnp.float32).astype(jnp.bfloat16)
        q_sums, k_sums, v_sums = [], [], []
        for h in range(n_kv):
            q_part = jnp.dot(
                chosen, q_weight[:, h * q_cols : (h + 1) * q_cols], preferred_element_type=jnp.float32
            ).astype(jnp.bfloat16)
            joined = jnp.concatenate(
                [q_part, k_part[:, h * k_cols : (h + 1) * k_cols], v_part[:, h * k_cols : (h + 1) * k_cols]],
                axis=1,
            )
            pieces = 2 if joined.shape[1] % 256 == 0 else 1
            piece = joined.shape[1] // pieces
            summed = jnp.concatenate(
                [
                    ring_reduce_scatter(
                        [
                            joined[k * block_rows : (k + 1) * block_rows, i * piece : (i + 1) * piece]
                            for k in range(n_row)
                        ]
                    )
                    for i in range(pieces)
                ],
                axis=1,
            )
            q_sums.append(summed[:, :q_cols])
            k_sums.append(summed[:, q_cols : q_cols + k_cols])
            v_sums.append(summed[:, q_cols + k_cols :])
        q_sum = jnp.concatenate(q_sums, axis=1)
        key_total_sum = jnp.concatenate(k_sums, axis=1)
        value_total_sum = jnp.concatenate(v_sums, axis=1)
        q_sum, late_slot_seq, late_row = lax.optimization_barrier((q_sum, slot_seq, row_index))
        starts = lookup(cache_len, sequences[:seq_dev])
        token_places = (starts[:, None] + jnp.arange(new_len)[None, :]).reshape(-1).astype(jnp.float32)
        row_total = q_sum.shape[0]
        queries = apply_turning(q_sum.reshape(row_total, -1, head_dim), token_places).astype(
            jnp.bfloat16
        )
        rotated_keys = apply_turning(
            key_total_sum.reshape(row_total, -1, head_dim), token_places
        ).astype(jnp.bfloat16)
        values = value_total_sum.reshape(row_total, -1, head_dim).astype(jnp.bfloat16)
        results = jax.vmap(attend)(
            queries.reshape(seq_dev, new_len, -1, head_dim),
            rotated_keys.reshape(seq_dev, new_len, -1, head_dim),
            values.reshape(seq_dev, new_len, -1, head_dim),
            k_cache,
            value_cache,
            starts,
        )
        attended = results.reshape(seq_dev * new_len, -1)
        n_gather = 4 if attended.shape[1] % 512 == 0 else n_kv
        gather_cols = attended.shape[1] // n_gather
        stacked = jnp.concatenate(
            [
                ring_all_gather(attended[:, i * gather_cols : (i + 1) * gather_cols])
                for i in range(n_gather)
            ],
            axis=1,
        )
        late_mine = jnp.arange(n_row, dtype=jnp.int32)[:, None] == late_row
        row_of_slot = jnp.sum(jnp.where(late_mine, jnp.asarray(stacked_table), 0), axis=0)
        seq_ids = jnp.arange(slot_total, dtype=jnp.int32)
        seq_base = jnp.sum(
            jnp.where(late_slot_seq[None, :] == seq_ids[:, None], row_of_slot[None, :], 0), axis=1
        )
        half = jnp.where(local < own_rows, 1 - col_index, col_index)
        t = half * own_rows + local % own_rows
        span_order = lookup(seq_base, t // new_len) + t % new_len
        arranged = jnp.dot(
            one_hot(span_order, span_rows), stacked, preferred_element_type=jnp.float32
        ).astype(jnp.bfloat16)
        arranged = lax.optimization_barrier(arranged)
        products = jnp.dot(arranged, o_weight, preferred_element_type=jnp.float32)
        received = lax.ppermute(products[:own_rows].astype(jnp.bfloat16), "col", [(0, 1), (1, 0)])
        return (products[own_rows:] + received.astype(jnp.float32)).astype(jnp.bfloat16)

    return body


def solution(mesh):
    return jax.shard_map(
        make_body(row_ring(mesh)),
        mesh=mesh,
        in_specs=(
            P(("groups", "col"), "row"),
            P("row", "col"),
            P("row", "col"),
            P("row", "col"),
            P("col", "row"),
            P(("groups", "row"), None, "col", None),
            P(("groups", "row"), None, "col", None),
            P("groups"),
            P("groups"),
        ),
        out_specs=P(("groups", "col"), "row"),
        check_vma=False,
    )
```

```python
import math

import jax
import jax.numpy as jnp
import numpy as np
from jax import lax
from jax.sharding import PartitionSpec as P

ROPE_BASE = 500000.0


def apply_turning(values, token_places):
    half_dim = values.shape[-1] // 2
    frequency = ROPE_BASE ** (-(2.0 * jnp.arange(half_dim, dtype=jnp.float32)) / values.shape[-1])
    angles = token_places[:, None] * frequency[None, :]
    cosine = jnp.cos(angles)[:, None, :]
    sine_part = jnp.sin(angles)[:, None, :]
    leading = values[..., :half_dim]
    trailing = values[..., half_dim:]
    return jnp.concatenate(
        [leading * cosine - trailing * sine_part, trailing * cosine + leading * sine_part], axis=-1
    )


def attend(queries, incoming_keys, incoming_values, cached_keys, cached_values, length):
    tokens_new, kv_heads, head_dim = incoming_keys.shape
    grouped = queries.reshape(tokens_new, kv_heads, -1, head_dim)
    scale_factor = 1.0 / math.sqrt(head_dim)
    cache_scores = (
        jnp.einsum("nkgd,ckd->kgnc", grouped, cached_keys, preferred_element_type=jnp.float32)
        * scale_factor
    )
    valid_cache = jnp.arange(cached_keys.shape[0]) < length
    cache_scores = jnp.where(valid_cache, cache_scores, -jnp.inf)
    fresh_scores = (
        jnp.einsum("nkgd,mkd->kgnm", grouped, incoming_keys, preferred_element_type=jnp.float32)
        * scale_factor
    )
    causal = jnp.arange(tokens_new)[None, :] <= jnp.arange(tokens_new)[:, None]
    fresh_scores = jnp.where(causal, fresh_scores, -jnp.inf)
    highest = jnp.maximum(jnp.max(cache_scores, axis=-1), jnp.max(fresh_scores, axis=-1))
    cache_weights = jnp.exp(cache_scores - highest[..., None])
    fresh_weights = jnp.exp(fresh_scores - highest[..., None])
    totals = jnp.sum(cache_weights, axis=-1) + jnp.sum(fresh_weights, axis=-1)
    weighted = jnp.einsum(
        "kgnc,ckd->nkgd",
        cache_weights.astype(jnp.bfloat16),
        cached_values,
        preferred_element_type=jnp.float32,
    )
    weighted = weighted + jnp.einsum(
        "kgnm,mkd->nkgd",
        fresh_weights.astype(jnp.bfloat16),
        incoming_values,
        preferred_element_type=jnp.float32,
    )
    normed = weighted / jnp.transpose(totals, (2, 0, 1))[..., None]
    return normed.reshape(tokens_new, -1).astype(jnp.bfloat16)


def row_ring(mesh):
    n_row = mesh.shape["row"]
    natural = list(range(n_row))
    try:
        names = list(mesh.axis_names)
        picked = np.moveaxis(np.asarray(mesh.devices), names.index("row"), 0).reshape(n_row, -1)[:, 0]
        coords = [tuple(d.coords) for d in picked]
    except Exception:
        return natural
    varying = [a for a in range(len(coords[0])) if len({c[a] for c in coords}) > 1]
    if len(varying) != 2:
        return natural
    sizes = {a: len({c[a] for c in coords}) for a in varying}
    inner = [a for a in varying if sizes[a] == 2]
    if not inner or sizes[varying[0]] * sizes[varying[1]] != n_row:
        return natural
    inner = inner[-1]
    outer = [a for a in varying if a != inner][0]
    lo, hi = min(c[inner] for c in coords), max(c[inner] for c in coords)
    first = sorted([i for i in natural if coords[i][inner] == lo], key=lambda i: coords[i][outer])
    second = sorted([i for i in natural if coords[i][inner] == hi], key=lambda i: -coords[i][outer])
    return first + second


def make_body(ring):
    n_row = len(ring)
    position_of = [ring.index(i) for i in range(n_row)]
    forward_hops = n_row // 2
    backward_hops = n_row - 1 - forward_hops
    forward_pairs = [(ring[i], ring[(i + 1) % n_row]) for i in range(n_row)]
    backward_pairs = [(ring[i], ring[(i - 1) % n_row]) for i in range(n_row)]
    gather_offsets = [0]
    for s in range(forward_hops):
        gather_offsets.append(-(s + 1) % n_row)
        if s < backward_hops:
            gather_offsets.append((s + 1) % n_row)
    stacked_of_offset = [gather_offsets.index(d) for d in range(n_row)]

    def tables(seq_dev, new_len):
        slots = np.zeros((n_row, n_row * seq_dev), np.int32)
        stacked_row = np.zeros((n_row, n_row * seq_dev), np.int32)
        for r in range(n_row):
            p = position_of[r]
            for k in range(n_row):
                for j in range(seq_dev):
                    slots[r, k * seq_dev + j] = ring[(p + k) % n_row] * seq_dev + j
            for slot in range(n_row * seq_dev):
                offset = (position_of[slot // seq_dev] - p) % n_row
                stacked_row[r, slot] = (stacked_of_offset[offset] * seq_dev + slot % seq_dev) * new_len
        return slots, stacked_row

    def add_bf16(a, b):
        return (a.astype(jnp.float32) + b.astype(jnp.float32)).astype(jnp.bfloat16)

    def ring_reduce_scatter(blocks):
        if n_row == 1:
            return blocks[0].astype(jnp.float32)
        forward = blocks[forward_hops % n_row]
        backward = blocks[(n_row - backward_hops) % n_row] if backward_hops else None
        got_forward = got_backward = None
        for s in range(forward_hops):
            got_forward = lax.ppermute(forward, "row", forward_pairs)
            if s < backward_hops:
                got_backward = lax.ppermute(backward, "row", backward_pairs)
            if s < forward_hops - 1:
                forward = add_bf16(got_forward, blocks[(forward_hops - s - 1) % n_row])
            if s < backward_hops - 1:
                backward = add_bf16(got_backward, blocks[(s + 1 - backward_hops) % n_row])
        total = got_forward.astype(jnp.float32) + blocks[0].astype(jnp.float32)
        if got_backward is not None:
            total = total + got_backward.astype(jnp.float32)
        return total

    def ring_all_gather(own):
        got = [own]
        forward = backward = own
        for s in range(forward_hops):
            forward = lax.ppermute(forward, "row", forward_pairs)
            got.append(forward)
            if s < backward_hops:
                backward = lax.ppermute(backward, "row", backward_pairs)
                got.append(backward)
        return jnp.concatenate(got, axis=0)

    def lookup(table, index):
        table = jnp.asarray(table, jnp.int32)
        hit = index[..., None] == jnp.arange(table.shape[0], dtype=jnp.int32)
        return jnp.sum(jnp.where(hit, table, 0), axis=-1)

    def one_hot(rows, width):
        return (rows[:, None] == jnp.arange(width, dtype=jnp.int32)[None, :]).astype(jnp.bfloat16)

    def body(
        tokens, q_weight, key_matrix, value_matrix, o_weight, k_cache, value_cache, cache_len, slot_seq
    ):
        row_index = lax.axis_index("row").astype(jnp.int32)
        col_index = lax.axis_index("col").astype(jnp.int32)
        n_col = 2
        seq_dev = k_cache.shape[0]
        head_dim = k_cache.shape[3]
        slot_total = slot_seq.shape[0]
        own_rows = tokens.shape[0]
        span_rows = own_rows * n_col
        new_len = span_rows // slot_total
        block_rows = seq_dev * new_len
        other_tokens = lax.ppermute(tokens, "col", [(0, 1), (1, 0)])
        slots_table, stacked_table = tables(seq_dev, new_len)
        mine_of_row = jnp.arange(n_row, dtype=jnp.int32)[:, None] == row_index
        slots = jnp.sum(jnp.where(mine_of_row, jnp.asarray(slots_table), 0), axis=0)
        sequences = lookup(slot_seq, slots)
        local = jnp.arange(span_rows, dtype=jnp.int32)
        token_rows = jnp.repeat(sequences, new_len) * new_len + local % new_len
        from_own = token_rows // own_rows == col_index
        in_half = token_rows % own_rows
        pick_own = one_hot(jnp.where(from_own, in_half, -1), own_rows)
        pick_other = one_hot(jnp.where(from_own, -1, in_half), own_rows)
        chosen = (
            jnp.dot(pick_own, tokens, preferred_element_type=jnp.float32)
            + jnp.dot(pick_other, other_tokens, preferred_element_type=jnp.float32)
        ).astype(jnp.bfloat16)
        n_kv = k_cache.shape[2]
        q_cols = q_weight.shape[1] // n_kv
        k_cols = key_matrix.shape[1] // n_kv
        k_part = jnp.dot(chosen, key_matrix, preferred_element_type=jnp.float32).astype(jnp.bfloat16)
        v_part = jnp.dot(chosen, value_matrix, preferred_element_type=jnp.float32).astype(jnp.bfloat16)
        q_all = jnp.dot(chosen, q_weight, preferred_element_type=jnp.float32).astype(jnp.bfloat16)
        q_sums, k_sums, v_sums = [], [], []
        for h in range(n_kv):
            q_part = q_all[:, h * q_cols : (h + 1) * q_cols]
            joined = jnp.concatenate(
                [q_part, k_part[:, h * k_cols : (h + 1) * k_cols], v_part[:, h * k_cols : (h + 1) * k_cols]],
                axis=1,
            )
            blocks = [joined[k * block_rows : (k + 1) * block_rows] for k in range(n_row)]
            summed = ring_reduce_scatter(blocks)
            q_sums.append(summed[:, :q_cols])
            k_sums.append(summed[:, q_cols : q_cols + k_cols])
            v_sums.append(summed[:, q_cols + k_cols :])
        q_sum = jnp.concatenate(q_sums, axis=1)
        key_total_sum = jnp.concatenate(k_sums, axis=1)
        value_total_sum = jnp.concatenate(v_sums, axis=1)
        q_sum, late_slot_seq, late_row = lax.optimization_barrier((q_sum, slot_seq, row_index))
        starts = lookup(cache_len, sequences[:seq_dev])
        token_places = (starts[:, None] + jnp.arange(new_len)[None, :]).reshape(-1).astype(jnp.float32)
        row_total = q_sum.shape[0]
        queries = apply_turning(q_sum.reshape(row_total, -1, head_dim), token_places).astype(
            jnp.bfloat16
        )
        rotated_keys = apply_turning(
            key_total_sum.reshape(row_total, -1, head_dim), token_places
        ).astype(jnp.bfloat16)
        values = value_total_sum.reshape(row_total, -1, head_dim).astype(jnp.bfloat16)
        results = jax.vmap(attend)(
            queries.reshape(seq_dev, new_len, -1, head_dim),
            rotated_keys.reshape(seq_dev, new_len, -1, head_dim),
            values.reshape(seq_dev, new_len, -1, head_dim),
            k_cache,
            value_cache,
            starts,
        )
        attended = results.reshape(seq_dev * new_len, -1)
        stacked = jnp.concatenate(
            [ring_all_gather(attended[:, h * q_cols : (h + 1) * q_cols]) for h in range(n_kv)], axis=1
        )
        late_mine = jnp.arange(n_row, dtype=jnp.int32)[:, None] == late_row
        row_of_slot = jnp.sum(jnp.where(late_mine, jnp.asarray(stacked_table), 0), axis=0)
        seq_ids = jnp.arange(slot_total, dtype=jnp.int32)
        seq_base = jnp.sum(
            jnp.where(late_slot_seq[None, :] == seq_ids[:, None], row_of_slot[None, :], 0), axis=1
        )
        half = jnp.where(local < own_rows, 1 - col_index, col_index)
        t = half * own_rows + local % own_rows
        span_order = lookup(seq_base, t // new_len) + t % new_len
        arranged = jnp.dot(
            one_hot(span_order, span_rows), stacked, preferred_element_type=jnp.float32
        ).astype(jnp.bfloat16)
        arranged = lax.optimization_barrier(arranged)
        products = jnp.dot(arranged, o_weight, preferred_element_type=jnp.float32)
        received = lax.ppermute(products[:own_rows].astype(jnp.bfloat16), "col", [(0, 1), (1, 0)])
        return (products[own_rows:] + received.astype(jnp.float32)).astype(jnp.bfloat16)

    return body


def solution(mesh):
    return jax.shard_map(
        make_body(row_ring(mesh)),
        mesh=mesh,
        in_specs=(
            P(("groups", "col"), "row"),
            P("row", "col"),
            P("row", "col"),
            P("row", "col"),
            P("col", "row"),
            P(("groups", "row"), None, "col", None),
            P(("groups", "row"), None, "col", None),
            P("groups"),
            P("groups"),
        ),
        out_specs=P(("groups", "col"), "row"),
        check_vma=False,
    )
```

```python
import math

import jax
import jax.numpy as jnp
import numpy as np
from jax import lax
from jax.sharding import PartitionSpec as P

ROPE_BASE = 500000.0


def apply_turning(values, token_places):
    half_dim = values.shape[-1] // 2
    frequency = ROPE_BASE ** (-(2.0 * jnp.arange(half_dim, dtype=jnp.float32)) / values.shape[-1])
    angles = token_places[:, None] * frequency[None, :]
    cosine = jnp.cos(angles)[:, None, :]
    sine_part = jnp.sin(angles)[:, None, :]
    leading = values[..., :half_dim]
    trailing = values[..., half_dim:]
    return jnp.concatenate(
        [leading * cosine - trailing * sine_part, trailing * cosine + leading * sine_part], axis=-1
    )


def attend(queries, incoming_keys, incoming_values, cached_keys, cached_values, length):
    tokens_new, kv_heads, head_dim = incoming_keys.shape
    grouped = queries.reshape(tokens_new, kv_heads, -1, head_dim)
    scale_factor = 1.0 / math.sqrt(head_dim)
    cache_scores = (
        jnp.einsum("nkgd,ckd->kgnc", grouped, cached_keys, preferred_element_type=jnp.float32)
        * scale_factor
    )
    valid_cache = jnp.arange(cached_keys.shape[0]) < length
    cache_scores = jnp.where(valid_cache, cache_scores, -jnp.inf)
    fresh_scores = (
        jnp.einsum("nkgd,mkd->kgnm", grouped, incoming_keys, preferred_element_type=jnp.float32)
        * scale_factor
    )
    causal = jnp.arange(tokens_new)[None, :] <= jnp.arange(tokens_new)[:, None]
    fresh_scores = jnp.where(causal, fresh_scores, -jnp.inf)
    highest = jnp.maximum(jnp.max(cache_scores, axis=-1), jnp.max(fresh_scores, axis=-1))
    cache_weights = jnp.exp(cache_scores - highest[..., None])
    fresh_weights = jnp.exp(fresh_scores - highest[..., None])
    totals = jnp.sum(cache_weights, axis=-1) + jnp.sum(fresh_weights, axis=-1)
    weighted = jnp.einsum(
        "kgnc,ckd->nkgd",
        cache_weights.astype(jnp.bfloat16),
        cached_values,
        preferred_element_type=jnp.float32,
    )
    weighted = weighted + jnp.einsum(
        "kgnm,mkd->nkgd",
        fresh_weights.astype(jnp.bfloat16),
        incoming_values,
        preferred_element_type=jnp.float32,
    )
    normed = weighted / jnp.transpose(totals, (2, 0, 1))[..., None]
    return normed.reshape(tokens_new, -1).astype(jnp.bfloat16)


def row_ring(mesh):
    n_row = mesh.shape["row"]
    natural = list(range(n_row))
    try:
        names = list(mesh.axis_names)
        picked = np.moveaxis(np.asarray(mesh.devices), names.index("row"), 0).reshape(n_row, -1)[:, 0]
        coords = [tuple(d.coords) for d in picked]
    except Exception:
        return natural
    varying = [a for a in range(len(coords[0])) if len({c[a] for c in coords}) > 1]
    if len(varying) != 2:
        return natural
    sizes = {a: len({c[a] for c in coords}) for a in varying}
    inner = [a for a in varying if sizes[a] == 2]
    if not inner or sizes[varying[0]] * sizes[varying[1]] != n_row:
        return natural
    inner = inner[-1]
    outer = [a for a in varying if a != inner][0]
    lo, hi = min(c[inner] for c in coords), max(c[inner] for c in coords)
    first = sorted([i for i in natural if coords[i][inner] == lo], key=lambda i: coords[i][outer])
    second = sorted([i for i in natural if coords[i][inner] == hi], key=lambda i: -coords[i][outer])
    return first + second


def make_body(ring):
    n_row = len(ring)
    position_of = [ring.index(i) for i in range(n_row)]
    forward_hops = n_row // 2
    backward_hops = n_row - 1 - forward_hops
    forward_pairs = [(ring[i], ring[(i + 1) % n_row]) for i in range(n_row)]
    backward_pairs = [(ring[i], ring[(i - 1) % n_row]) for i in range(n_row)]
    gather_offsets = [0]
    for s in range(forward_hops):
        gather_offsets.append(-(s + 1) % n_row)
        if s < backward_hops:
            gather_offsets.append((s + 1) % n_row)
    stacked_of_offset = [gather_offsets.index(d) for d in range(n_row)]

    def tables(seq_dev, new_len):
        slots = np.zeros((n_row, n_row * seq_dev), np.int32)
        stacked_row = np.zeros((n_row, n_row * seq_dev), np.int32)
        for r in range(n_row):
            p = position_of[r]
            for k in range(n_row):
                for j in range(seq_dev):
                    slots[r, k * seq_dev + j] = ring[(p + k) % n_row] * seq_dev + j
            for slot in range(n_row * seq_dev):
                offset = (position_of[slot // seq_dev] - p) % n_row
                stacked_row[r, slot] = ((slot % seq_dev) * n_row + stacked_of_offset[offset]) * new_len
        return slots, stacked_row

    def add_bf16(a, b):
        return (a.astype(jnp.float32) + b.astype(jnp.float32)).astype(jnp.bfloat16)

    def ring_reduce_scatter(blocks):
        if n_row == 1:
            return blocks[0].astype(jnp.float32)
        forward = blocks[forward_hops % n_row]
        backward = blocks[(n_row - backward_hops) % n_row] if backward_hops else None
        got_forward = got_backward = None
        for s in range(forward_hops):
            got_forward = lax.ppermute(forward, "row", forward_pairs)
            if s < backward_hops:
                got_backward = lax.ppermute(backward, "row", backward_pairs)
            if s < forward_hops - 1:
                forward = add_bf16(got_forward, blocks[(forward_hops - s - 1) % n_row])
            if s < backward_hops - 1:
                backward = add_bf16(got_backward, blocks[(s + 1 - backward_hops) % n_row])
        total = got_forward.astype(jnp.float32) + blocks[0].astype(jnp.float32)
        if got_backward is not None:
            total = total + got_backward.astype(jnp.float32)
        return total

    def ring_all_gather(own):
        got = [own]
        forward = backward = own
        for s in range(forward_hops):
            forward = lax.ppermute(forward, "row", forward_pairs)
            got.append(forward)
            if s < backward_hops:
                backward = lax.ppermute(backward, "row", backward_pairs)
                got.append(backward)
        return jnp.concatenate(got, axis=0)

    def lookup(table, index):
        table = jnp.asarray(table, jnp.int32)
        hit = index[..., None] == jnp.arange(table.shape[0], dtype=jnp.int32)
        return jnp.sum(jnp.where(hit, table, 0), axis=-1)

    def one_hot(rows, width):
        return (rows[:, None] == jnp.arange(width, dtype=jnp.int32)[None, :]).astype(jnp.bfloat16)

    def body(
        tokens, q_weight, key_matrix, value_matrix, o_weight, k_cache, value_cache, cache_len, slot_seq
    ):
        row_index = lax.axis_index("row").astype(jnp.int32)
        col_index = lax.axis_index("col").astype(jnp.int32)
        n_col = 2
        seq_dev = k_cache.shape[0]
        head_dim = k_cache.shape[3]
        slot_total = slot_seq.shape[0]
        own_rows = tokens.shape[0]
        span_rows = own_rows * n_col
        new_len = span_rows // slot_total
        block_rows = seq_dev * new_len
        other_tokens = lax.ppermute(tokens, "col", [(0, 1), (1, 0)])
        slots_table, stacked_table = tables(seq_dev, new_len)
        mine_of_row = jnp.arange(n_row, dtype=jnp.int32)[:, None] == row_index
        slots = jnp.sum(jnp.where(mine_of_row, jnp.asarray(slots_table), 0), axis=0)
        sequences = lookup(slot_seq, slots)
        local = jnp.arange(span_rows, dtype=jnp.int32)
        token_rows = jnp.repeat(sequences, new_len) * new_len + local % new_len
        from_own = token_rows // own_rows == col_index
        in_half = token_rows % own_rows
        pick_own = one_hot(jnp.where(from_own, in_half, -1), own_rows)
        pick_other = one_hot(jnp.where(from_own, -1, in_half), own_rows)
        chosen = (
            jnp.dot(pick_own, tokens, preferred_element_type=jnp.float32)
            + jnp.dot(pick_other, other_tokens, preferred_element_type=jnp.float32)
        ).astype(jnp.bfloat16)
        q_part = jnp.dot(chosen, q_weight, preferred_element_type=jnp.float32).astype(jnp.bfloat16)
        k_part = jnp.dot(chosen, key_matrix, preferred_element_type=jnp.float32).astype(jnp.bfloat16)
        v_part = jnp.dot(chosen, value_matrix, preferred_element_type=jnp.float32).astype(jnp.bfloat16)
        q_cols = q_part.shape[1]
        k_cols = k_part.shape[1]
        joined = jnp.concatenate([q_part, k_part, v_part], axis=1)
        starts = lookup(cache_len, sequences[:seq_dev])
        gathered = []
        late = None
        for j in range(seq_dev):
            blocks = [
                joined[k * block_rows + j * new_len : k * block_rows + (j + 1) * new_len] for k in range(n_row)
            ]
            summed = ring_reduce_scatter(blocks)
            if late is None:
                summed, late_slot_seq, late_row = lax.optimization_barrier((summed, slot_seq, row_index))
                late = True
            token_places = (starts[j] + jnp.arange(new_len)).astype(jnp.float32)
            queries = apply_turning(summed[:, :q_cols].reshape(new_len, -1, head_dim), token_places).astype(
                jnp.bfloat16
            )
            rotated_keys = apply_turning(
                summed[:, q_cols : q_cols + k_cols].reshape(new_len, -1, head_dim), token_places
            ).astype(jnp.bfloat16)
            values = summed[:, q_cols + k_cols :].reshape(new_len, -1, head_dim).astype(jnp.bfloat16)
            attended = attend(queries, rotated_keys, values, k_cache[j], value_cache[j], starts[j])
            gathered.append(ring_all_gather(attended))
        stacked = jnp.concatenate(gathered, axis=0)
        late_mine = jnp.arange(n_row, dtype=jnp.int32)[:, None] == late_row
        row_of_slot = jnp.sum(jnp.where(late_mine, jnp.asarray(stacked_table), 0), axis=0)
        seq_ids = jnp.arange(slot_total, dtype=jnp.int32)
        seq_base = jnp.sum(
            jnp.where(late_slot_seq[None, :] == seq_ids[:, None], row_of_slot[None, :], 0), axis=1
        )
        half = jnp.where(local < own_rows, 1 - col_index, col_index)
        t = half * own_rows + local % own_rows
        span_order = lookup(seq_base, t // new_len) + t % new_len
        arranged = jnp.dot(
            one_hot(span_order, span_rows), stacked, preferred_element_type=jnp.float32
        ).astype(jnp.bfloat16)
        arranged = lax.optimization_barrier(arranged)
        products = jnp.dot(arranged, o_weight, preferred_element_type=jnp.float32)
        received = lax.ppermute(products[:own_rows].astype(jnp.bfloat16), "col", [(0, 1), (1, 0)])
        return (products[own_rows:] + received.astype(jnp.float32)).astype(jnp.bfloat16)

    return body


def solution(mesh):
    return jax.shard_map(
        make_body(row_ring(mesh)),
        mesh=mesh,
        in_specs=(
            P(("groups", "col"), "row"),
            P("row", "col"),
            P("row", "col"),
            P("row", "col"),
            P("col", "row"),
            P(("groups", "row"), None, "col", None),
            P(("groups", "row"), None, "col", None),
            P("groups"),
            P("groups"),
        ),
        out_specs=P(("groups", "col"), "row"),
        check_vma=False,
    )
```
